32 devices in a mesh: groups: 2 (over x), blk: 16 (over z, y, core).
Axes of the slice: x: 2, y: 2, z: 4, core: 2. Of those that a mesh axis runs over, the one named last changes fastest.
Arguments:
- embeddings: bfloat16 [30720, 1024], P(('groups', 'blk')), parts along dimension 0, may hold values from -6 to 6
- owners: int32 [30720], P(('groups', 'blk')), parts along dimension 0, may hold values from 0 to 15, as said below
- clusters: int32 [30720], P(('groups', 'blk')), parts along dimension 0, may hold values from 0 to 15
- pairs: int32 [32, 4, 8, 4], P(('groups', 'blk')), parts along dimension 0, may hold values from 0 to 8
Outputs:
- scores: float32 [30720], P(('groups', 'blk')), parts along dimension 0
The draws below stay inside these ranges and needn't reach their ends.
There are 2 independent parts, one for each index of `groups`. The reference program is written for one: setup_inputs(seed, part) draws one part's arguments, and reference() takes and returns one part's arrays. A program takes and returns all parts, laid end to end along the dimension named above; each array names one. Nothing has to cross between parts.
Inputs may be any that keep to these rules, and one draw needn't show every extreme that they name: `owners`: each device sends at most 64 of its rows to one owner; in every draw one owner receives exactly 64 rows from every device.
All inputs are finite; a program needn't handle non-finite values.
Results may differ from the reference program's by a relative error of at most 0.0003.
Values may be sent and summed in bfloat16 or wider, within the bound.
No kernel may reach another device: no remote copies, remote signals or barrier semaphores. Data moves between devices by JAX's collectives and lax.ppermute only.
A program may use at most 64 MiB of HBM per device.

```python
import jax
import jax.numpy as jnp
from jax import lax

FEATURE_LENGTH = 1024
SLOTS = 1024
STEPS = 4
PARTNERS = 4
CLUSTERS = 16
ROWS = 960
BLOCKS = 8
CAP = 64
N_BLK = 16


def draw_owners(key, part):
    hot_owner = jax.random.randint(jax.random.fold_in(key, 7), (), 0, N_BLK)
    slot_owner = (jnp.arange(N_BLK * CAP, dtype=jnp.int32) // CAP).astype(jnp.int32)

    def one_source(source):
        source_key = jax.random.fold_in(key, source + 11)
        order = jax.random.permutation(source_key, N_BLK * CAP).astype(jnp.int32)
        sorted_positions = order + jnp.where(slot_owner == hot_owner, N_BLK * CAP, 0).astype(jnp.int32)
        selected_tiles = lax.top_k(sorted_positions, ROWS)[1]
        picked = slot_owner[selected_tiles]
        return jax.random.permutation(jax.random.fold_in(source_key, 3), picked)
    return jax.vmap(one_source)(jnp.arange(N_BLK, dtype=jnp.int32)).reshape(-1).astype(jnp.int32)


def with_ends(entries, rng, least, top_value):
    index_at = [jax.random.randint(jax.random.fold_in(rng, axis), (), 0, length) for axis, length in enumerate(entries.shape)]
    widest = entries.shape.index(max(entries.shape))
    next_to = index_at[:widest] + [(index_at[widest] + 1) % entries.shape[widest]] + index_at[widest + 1:]
    return entries.at[tuple(index_at)].set(least).at[tuple(next_to)].set(top_value)


def level_of(own_key, extent, split, low, top_value):
    loudness, own = 1.0, jax.random.fold_in(own_key, 6)
    for axis_at, shards_of in split:
        steps = jnp.exp(jax.random.uniform(jax.random.fold_in(own, axis_at), (shards_of,), jnp.float32, low / len(split), top_value / len(split)))
        loudness = loudness * jnp.repeat(steps, extent[axis_at] // shards_of).reshape([-1 if axis == axis_at else 1 for axis in range(len(extent))])
    return loudness


def centred(stream_key, dims, scale, reach, cuts=(), held_as=jnp.bfloat16):
    factor_of = level_of(stream_key, dims, cuts, -0.22, 0.18) if cuts else 1.0
    result = jax.random.normal(stream_key, dims, jnp.float32) * scale * factor_of
    return jnp.minimum(jnp.maximum(result, -reach), reach).astype(held_as)


def setup_inputs(seed: int = 0, part: int = 0) -> dict:
    keys = jax.random.split(jax.random.key(seed), 5)
    part_splits = jax.random.split(jax.random.fold_in(keys[4], part), 5)
    return {
        "embeddings": centred(part_splits[0], (N_BLK * ROWS, FEATURE_LENGTH), 1.0, 6.0, ((0, 16),)),
        "owners": draw_owners(jax.random.fold_in(jax.random.fold_in(keys[4], part), 71), part),
        "clusters": with_ends(jax.random.randint(part_splits[2], (N_BLK * ROWS,), 0, CLUSTERS), jax.random.fold_in(part_splits[2], 1), 0, CLUSTERS - 1).astype(jnp.int32),
        "pairs": with_ends(jax.random.randint(part_splits[3], (N_BLK, STEPS, BLOCKS, PARTNERS), 0, BLOCKS + 1), jax.random.fold_in(part_splits[3], 1), 0, BLOCKS).astype(jnp.int32),
    }


SHARPNESS_KNOB = 32.0

def landing_sequence(owners, device_count):
    onehot = (owners[..., None] == jnp.arange(device_count, dtype=jnp.int32)).astype(jnp.int32)
    prior_rows = jnp.cumsum(onehot, axis=-2) - onehot
    return lax.optimization_barrier(jnp.sum(prior_rows * onehot, axis=-1)).astype(jnp.int32)

def reference(embeddings, owners, clusters, pairs):
    value_entries = embeddings.astype(jnp.float32)
    unit = (value_entries * lax.rsqrt(lax.optimization_barrier(jnp.mean(value_entries * value_entries, axis=1, keepdims=True)) + 1e-06)).astype(jnp.bfloat16)
    capacity = SLOTS // N_BLK
    arrival = landing_sequence(owners.reshape(N_BLK, ROWS), N_BLK).reshape(-1)
    source = (jnp.arange(N_BLK * ROWS, dtype=jnp.int32) // ROWS).astype(jnp.int32)
    place = (owners * SLOTS + source * capacity + arrival).astype(jnp.int32)
    held = jnp.zeros((N_BLK * SLOTS, FEATURE_LENGTH), jnp.bfloat16).at[place].set(unit).reshape(N_BLK, BLOCKS, 128, FEATURE_LENGTH)
    held_ids = jnp.full((N_BLK * SLOTS,), -1, jnp.int32).at[place].set(clusters).reshape(N_BLK, BLOCKS, 128)
    diagonal = jnp.eye(128, dtype=bool)
    block_index = jnp.arange(BLOCKS, dtype=jnp.int32)
    reciprocal_factor = SHARPNESS_KNOB / FEATURE_LENGTH

    def owner_score(owner):
        local = held[owner].astype(jnp.float32)
        local_ids = held_ids[owner]
        total = jnp.zeros((BLOCKS, 128), jnp.float32)
        for cycle_step in range(STEPS):
            sender = ((owner - cycle_step) % N_BLK).astype(jnp.int32)
            remote = held[sender]
            remote_ids = held_ids[sender]
            for which in range(PARTNERS):
                partner = pairs[owner, cycle_step, :, which]
                live = partner < BLOCKS
                pick = jnp.minimum(partner, BLOCKS - 1).astype(jnp.int32)
                tiles = remote[pick].astype(jnp.float32)
                block_labels = remote_ids[pick]
                logits = jnp.einsum('bid,bjd->bij', local, tiles) * reciprocal_factor
                keep = live[:, None, None] & (local_ids[:, :, None] == block_labels[:, None, :]) & (local_ids[:, :, None] >= 0)
                if cycle_step == 0:
                    keep = keep & jnp.logical_not((pick == block_index)[:, None, None] & diagonal)
                total = total + lax.optimization_barrier(jnp.sum(jnp.where(keep, jnp.exp(logits), jnp.zeros_like(logits)), axis=2))
        return jnp.log1p(total)
    slot_scores = lax.map(owner_score, jnp.arange(N_BLK, dtype=jnp.int32))
    return slot_scores.reshape(-1)[place]
```

```python
import numpy as np
import jax
import jax.numpy as jnp
from jax import lax
from jax.sharding import PartitionSpec as P

SLOTS = 1024
STEPS = 4
ID_ROWS = 16


SHARPNESS_KNOB = 32.0


def ring_order(n):
    if n == 16:
        chips = [(z, 0) for z in range(4)] + [(z, 1) for z in reversed(range(4))]
        return [chips[p // 2][0] * 4 + chips[p // 2][1] * 2 + p % 2 for p in range(n)]
    return list(range(n))


def moved(x, pos2dev, moves):
    return lax.ppermute(x, "blk", [(pos2dev[a], pos2dev[b]) for a, b in moves])


def step_total(local, local_ids, remote, remote_ids, step_pairs, first_step):
    slot_count, feature_span = local.shape
    block_count = slot_count // 128
    logits = lax.dot_general(
        local, remote, (((1,), (1,)), ((), ())), preferred_element_type=jnp.float32
    ) * (SHARPNESS_KNOB / feature_span)
    keep = (local_ids[:, None] == remote_ids[None, :]) & (local_ids[:, None] >= 0)
    if first_step:
        keep = keep & jnp.logical_not(jnp.eye(slot_count, dtype=bool))
    contrib = jnp.where(keep, jnp.exp(logits), 0.0)
    per_block = contrib.reshape(slot_count, block_count, 128).sum(axis=2)
    counts = jnp.sum(
        step_pairs[:, :, None] == jnp.arange(block_count, dtype=jnp.int32), axis=1
    ).astype(jnp.float32)
    per_block = per_block.reshape(block_count, 128, block_count)
    return jnp.sum(per_block * counts[:, None, :], axis=2)


def pack(held, held_ids):
    feature_span = held.shape[1]
    id_rows = jnp.pad(held_ids.astype(jnp.bfloat16), (0, ID_ROWS * feature_span - held_ids.shape[0]))
    return jnp.concatenate([held, id_rows.reshape(ID_ROWS, feature_span)], axis=0)


def unpack(packed):
    slot_count = packed.shape[0] - ID_ROWS
    return packed[:slot_count], packed[slot_count:].reshape(-1)[:slot_count].astype(jnp.int32)


def body(embeddings, owners, clusters, pairs):
    device_count = lax.axis_size("blk")
    row_count, feature_span = embeddings.shape
    slot_count = SLOTS
    capacity = slot_count // device_count
    block_count = slot_count // 128
    pos2dev = ring_order(device_count)
    dev2pos = np.argsort(np.asarray(pos2dev)).astype(np.int32)
    position = jnp.asarray(dev2pos)[lax.axis_index("blk")]
    odd = (position % 2) == 1

    value_entries = embeddings.astype(jnp.float32)
    unit = (
        value_entries
        * lax.rsqrt(jnp.mean(value_entries * value_entries, axis=1, keepdims=True) + 1e-06)
    ).astype(jnp.bfloat16)
    row_index = jnp.arange(row_count, dtype=jnp.int32)
    earlier = (owners[None, :] == owners[:, None]) & (row_index[None, :] < row_index[:, None])
    arrival = jnp.sum(earlier.astype(jnp.int32), axis=1)
    place = jnp.asarray(np.asarray(pos2dev, np.int32))[owners] * capacity + arrival
    slot_index = jnp.arange(slot_count, dtype=jnp.int32)
    hit = place[None, :] == slot_index[:, None]
    outgoing = jnp.dot(
        hit.astype(jnp.bfloat16), unit, preferred_element_type=jnp.float32
    ).astype(jnp.bfloat16)
    outgoing_ids = jnp.sum(jnp.where(hit, clusters[None, :] + 1, 0), axis=1) - 1
    id_row = jnp.pad(
        outgoing_ids.reshape(device_count, 1, capacity).astype(jnp.bfloat16),
        ((0, 0), (0, 0), (0, feature_span - capacity)),
    )
    payload = jnp.concatenate([outgoing.reshape(device_count, capacity, feature_span), id_row], axis=1)
    arrived = lax.all_to_all(payload, "blk", split_axis=0, concat_axis=0, tiled=True)
    own = arrived[:, :capacity].reshape(slot_count, feature_span)
    own_ids = arrived[:, capacity, :capacity].reshape(slot_count).astype(jnp.int32)

    all_pairs = lax.all_gather(pairs[0], "blk", axis=0, tiled=False)
    my_pairs = all_pairs[position]
    ahead_pairs = all_pairs[(position + 2) % device_count]

    n = device_count
    evens = range(0, n, 2)
    packed = pack(own, own_ids)
    back2 = moved(packed, pos2dev, [(p, (p - 2) % n) for p in evens])
    fwd2 = moved(packed, pos2dev, [(p, (p + 2) % n) for p in range(n)])
    across = moved(packed, pos2dev, [(p, p + 1) for p in evens])
    fwd2_swapped = moved(fwd2, pos2dev, [(p, p ^ 1) for p in range(n)])
    back2_held, back2_ids = unpack(back2)
    fwd2_held, fwd2_ids = unpack(fwd2)
    across_held, across_ids = unpack(across)
    swapped_held, swapped_ids = unpack(fwd2_swapped)

    total = step_total(own, own_ids, own, own_ids, my_pairs[0], True)
    total = total + step_total(
        own,
        own_ids,
        jnp.where(odd, across_held, swapped_held),
        jnp.where(odd, across_ids, swapped_ids),
        my_pairs[1],
        False,
    )
    total = total + step_total(own, own_ids, fwd2_held, fwd2_ids, my_pairs[2], False)
    last = step_total(
        jnp.where(odd, own, back2_held),
        jnp.where(odd, own_ids, back2_ids),
        swapped_held,
        swapped_ids,
        jnp.where(odd, my_pairs[3], ahead_pairs[3]),
        False,
    )
    handed = moved(last, pos2dev, [(p, (p + 2) % n) for p in evens])
    total = total + jnp.where(odd, last, handed)

    slot_scores = jnp.log1p(total).reshape(device_count, capacity)
    returned = lax.all_to_all(slot_scores, "blk", split_axis=0, concat_axis=0, tiled=True).reshape(-1)
    return jnp.sum(jnp.where(place[:, None] == slot_index[None, :], returned[None, :], 0.0), axis=1)


def solution(mesh):
    placed = (
        P(("groups", "blk"), None),
        P(("groups", "blk")),
        P(("groups", "blk")),
        P(("groups", "blk"), None, None, None),
    )
    return jax.shard_map(
        body, mesh=mesh, in_specs=placed, out_specs=P(("groups", "blk")), check_vma=False
    )
```

```python
import numpy as np
import jax
import jax.numpy as jnp
from jax import lax
from jax.sharding import PartitionSpec as P

SLOTS = 1024
STEPS = 4
ID_ROWS = 16


SHARPNESS_KNOB = 32.0


def ring_order(n):
    if n == 16:
        chips = [(z, 0) for z in range(4)] + [(z, 1) for z in reversed(range(4))]
        return [chips[p // 2][0] * 4 + chips[p // 2][1] * 2 + p % 2 for p in range(n)]
    return list(range(n))


def moved(x, pos2dev, moves):
    return lax.ppermute(x, "blk", [(pos2dev[a], pos2dev[b]) for a, b in moves])


def step_total(local, local_ids, remote, remote_ids, step_pairs, first_step):
    slot_count, feature_span = local.shape
    block_count = slot_count // 128
    logits = lax.dot_general(
        local, remote, (((1,), (1,)), ((), ())), preferred_element_type=jnp.float32
    ) * (SHARPNESS_KNOB / feature_span)
    keep = (local_ids[:, None] == remote_ids[None, :]) & (local_ids[:, None] >= 0)
    if first_step:
        keep = keep & jnp.logical_not(jnp.eye(slot_count, dtype=bool))
    contrib = jnp.where(keep, jnp.exp(logits), 0.0)
    per_block = contrib.reshape(slot_count, block_count, 128).sum(axis=2)
    counts = jnp.sum(
        step_pairs[:, :, None] == jnp.arange(block_count, dtype=jnp.int32), axis=1
    ).astype(jnp.float32)
    per_block = per_block.reshape(block_count, 128, block_count)
    return jnp.sum(per_block * counts[:, None, :], axis=2)


def pack(held, held_ids):
    feature_span = held.shape[1]
    id_rows = jnp.pad(held_ids.astype(jnp.bfloat16), (0, ID_ROWS * feature_span - held_ids.shape[0]))
    return jnp.concatenate([held, id_rows.reshape(ID_ROWS, feature_span)], axis=0)


def unpack(packed):
    slot_count = packed.shape[0] - ID_ROWS
    return packed[:slot_count], packed[slot_count:].reshape(-1)[:slot_count].astype(jnp.int32)


def body(embeddings, owners, clusters, pairs):
    device_count = lax.axis_size("blk")
    row_count, feature_span = embeddings.shape
    slot_count = SLOTS
    capacity = slot_count // device_count
    block_count = slot_count // 128
    pos2dev = ring_order(device_count)
    dev2pos = np.argsort(np.asarray(pos2dev)).astype(np.int32)
    position = jnp.asarray(dev2pos)[lax.axis_index("blk")]
    odd = (position % 2) == 1

    value_entries = embeddings.astype(jnp.float32)
    unit = (
        value_entries
        * lax.rsqrt(jnp.mean(value_entries * value_entries, axis=1, keepdims=True) + 1e-06)
    ).astype(jnp.bfloat16)
    row_index = jnp.arange(row_count, dtype=jnp.int32)
    earlier = (owners[None, :] == owners[:, None]) & (row_index[None, :] < row_index[:, None])
    arrival = jnp.sum(earlier.astype(jnp.int32), axis=1)
    place = jnp.asarray(np.asarray(pos2dev, np.int32))[owners] * capacity + arrival
    slot_index = jnp.arange(slot_count, dtype=jnp.int32)
    hit = place[None, :] == slot_index[:, None]
    outgoing = jnp.dot(
        hit.astype(jnp.bfloat16), unit, preferred_element_type=jnp.float32
    ).astype(jnp.bfloat16)
    outgoing_ids = jnp.sum(jnp.where(hit, clusters[None, :] + 1, 0), axis=1) - 1
    pair_count = pairs[0].size
    side = jnp.concatenate(
        [
            outgoing_ids.reshape(device_count, capacity),
            jnp.broadcast_to(pairs[0].reshape(1, pair_count), (device_count, pair_count)),
        ],
        axis=1,
    ).astype(jnp.bfloat16)
    id_row = jnp.pad(side, ((0, 0), (0, feature_span - capacity - pair_count)))[:, None, :]
    payload = jnp.concatenate([outgoing.reshape(device_count, capacity, feature_span), id_row], axis=1)
    arrived = lax.all_to_all(payload, "blk", split_axis=0, concat_axis=0, tiled=True)
    own = arrived[:, :capacity].reshape(slot_count, feature_span)
    own_ids = arrived[:, capacity, :capacity].reshape(slot_count).astype(jnp.int32)

    all_pairs = (
        arrived[:, capacity, capacity : capacity + pair_count].astype(jnp.int32).reshape((device_count,) + pairs.shape[1:])
    )
    my_pairs = all_pairs[position]
    ahead_pairs = all_pairs[(position + 2) % device_count]

    n = device_count
    evens = range(0, n, 2)
    packed = pack(own, own_ids)
    back2 = moved(packed, pos2dev, [(p, (p - 2) % n) for p in evens])
    fwd2 = moved(packed, pos2dev, [(p, (p + 2) % n) for p in range(n)])
    across = moved(packed, pos2dev, [(p, p + 1) for p in evens])
    total = step_total(own, own_ids, own, own_ids, my_pairs[0], True)
    total, back2, fwd2, across = lax.optimization_barrier((total, back2, fwd2, across))
    fwd2_swapped = moved(fwd2, pos2dev, [(p, p ^ 1) for p in range(n)])
    back2_held, back2_ids = unpack(back2)
    fwd2_held, fwd2_ids = unpack(fwd2)
    across_held, across_ids = unpack(across)
    swapped_held, swapped_ids = unpack(fwd2_swapped)

    total = total + step_total(
        own,
        own_ids,
        jnp.where(odd, across_held, swapped_held),
        jnp.where(odd, across_ids, swapped_ids),
        my_pairs[1],
        False,
    )
    total = total + step_total(own, own_ids, fwd2_held, fwd2_ids, my_pairs[2], False)
    last = step_total(
        jnp.where(odd, own, back2_held),
        jnp.where(odd, own_ids, back2_ids),
        swapped_held,
        swapped_ids,
        jnp.where(odd, my_pairs[3], ahead_pairs[3]),
        False,
    )
    handed = moved(last, pos2dev, [(p, (p + 2) % n) for p in evens])
    total = total + jnp.where(odd, last, handed)

    slot_scores = jnp.log1p(total).reshape(device_count, capacity)
    returned = lax.all_to_all(slot_scores, "blk", split_axis=0, concat_axis=0, tiled=True).reshape(-1)
    return jnp.sum(jnp.where(place[:, None] == slot_index[None, :], returned[None, :], 0.0), axis=1)


def solution(mesh):
    placed = (
        P(("groups", "blk"), None),
        P(("groups", "blk")),
        P(("groups", "blk")),
        P(("groups", "blk"), None, None, None),
    )
    return jax.shard_map(
        body, mesh=mesh, in_specs=placed, out_specs=P(("groups", "blk")), check_vma=False
    )
```

```python
import numpy as np
import jax
import jax.numpy as jnp
from jax import lax
from jax.sharding import PartitionSpec as P

SLOTS = 1024
STEPS = 4
ID_ROWS = 16


SHARPNESS_KNOB = 32.0


def ring_order(n):
    if n == 16:
        chips = [(z, 0) for z in range(4)] + [(z, 1) for z in reversed(range(4))]
        return [chips[p // 2][0] * 4 + chips[p // 2][1] * 2 + p % 2 for p in range(n)]
    return list(range(n))


def moved(x, pos2dev, moves):
    return lax.ppermute(x, "blk", [(pos2dev[a], pos2dev[b]) for a, b in moves])


def step_total(local, local_ids, remote, remote_ids, step_pairs, first_step):
    slot_count, feature_span = local.shape
    block_count = slot_count // 128
    logits = lax.dot_general(
        local, remote, (((1,), (1,)), ((), ())), preferred_element_type=jnp.float32
    ) * (SHARPNESS_KNOB / feature_span)
    keep = (local_ids[:, None] == remote_ids[None, :]) & (local_ids[:, None] >= 0)
    if first_step:
        keep = keep & jnp.logical_not(jnp.eye(slot_count, dtype=bool))
    contrib = jnp.where(keep, jnp.exp(logits), 0.0)
    per_block = contrib.reshape(slot_count, block_count, 128).sum(axis=2)
    counts = jnp.sum(
        step_pairs[:, :, None] == jnp.arange(block_count, dtype=jnp.int32), axis=1
    ).astype(jnp.float32)
    per_block = per_block.reshape(block_count, 128, block_count)
    return jnp.sum(per_block * counts[:, None, :], axis=2)


def pack(held, held_ids):
    feature_span = held.shape[1]
    id_rows = jnp.pad(held_ids.astype(jnp.bfloat16), (0, ID_ROWS * feature_span - held_ids.shape[0]))
    return jnp.concatenate([held, id_rows.reshape(ID_ROWS, feature_span)], axis=0)


def unpack(packed):
    slot_count = packed.shape[0] - ID_ROWS
    return packed[:slot_count], packed[slot_count:].reshape(-1)[:slot_count].astype(jnp.int32)


def body(embeddings, owners, clusters, pairs):
    device_count = lax.axis_size("blk")
    row_count, feature_span = embeddings.shape
    slot_count = SLOTS
    capacity = slot_count // device_count
    block_count = slot_count // 128
    pos2dev = ring_order(device_count)
    dev2pos = np.argsort(np.asarray(pos2dev)).astype(np.int32)
    position = jnp.asarray(dev2pos)[lax.axis_index("blk")]
    odd = (position % 2) == 1

    value_entries = embeddings.astype(jnp.float32)
    unit = (
        value_entries
        * lax.rsqrt(jnp.mean(value_entries * value_entries, axis=1, keepdims=True) + 1e-06)
    ).astype(jnp.bfloat16)
    row_index = jnp.arange(row_count, dtype=jnp.int32)
    earlier = (owners[None, :] == owners[:, None]) & (row_index[None, :] < row_index[:, None])
    arrival = jnp.sum(earlier.astype(jnp.int32), axis=1)
    place = jnp.asarray(np.asarray(pos2dev, np.int32))[owners] * capacity + arrival
    slot_index = jnp.arange(slot_count, dtype=jnp.int32)
    hit = place[None, :] == slot_index[:, None]
    outgoing = jnp.dot(
        hit.astype(jnp.bfloat16), unit, preferred_element_type=jnp.float32
    ).astype(jnp.bfloat16)
    outgoing_ids = jnp.sum(jnp.where(hit, clusters[None, :] + 1, 0), axis=1) - 1
    pair_count = pairs[0].size
    side = jnp.concatenate(
        [
            outgoing_ids.reshape(device_count, capacity),
            jnp.broadcast_to(pairs[0].reshape(1, pair_count), (device_count, pair_count)),
        ],
        axis=1,
    ).astype(jnp.bfloat16)
    id_row = jnp.pad(side, ((0, 0), (0, feature_span - capacity - pair_count)))[:, None, :]
    payload = jnp.concatenate([outgoing.reshape(device_count, capacity, feature_span), id_row], axis=1)
    arrived = lax.all_to_all(payload, "blk", split_axis=0, concat_axis=0, tiled=True)
    own = arrived[:, :capacity].reshape(slot_count, feature_span)
    own_ids = arrived[:, capacity, :capacity].reshape(slot_count).astype(jnp.int32)

    all_pairs = (
        arrived[:, capacity, capacity : capacity + pair_count].astype(jnp.int32).reshape((device_count,) + pairs.shape[1:])
    )
    my_pairs = all_pairs[position]
    ahead_pairs = all_pairs[(position + 2) % device_count]

    n = device_count
    evens = range(0, n, 2)
    packed = pack(own, own_ids)
    back2 = moved(packed, pos2dev, [(p, (p - 2) % n) for p in evens])
    fwd2 = moved(packed, pos2dev, [(p, (p + 2) % n) for p in range(n)])
    across = moved(packed, pos2dev, [(p, p + 1) for p in evens])
    total = step_total(own, own_ids, own, own_ids, my_pairs[0], True)
    total, back2, fwd2, across = lax.optimization_barrier((total, back2, fwd2, across))
    fwd2_swapped = moved(fwd2, pos2dev, [(p, p ^ 1) for p in range(n)])
    back2_held, back2_ids = unpack(back2)
    fwd2_held, fwd2_ids = unpack(fwd2)
    across_held, across_ids = unpack(across)
    swapped_held, swapped_ids = unpack(fwd2_swapped)

    total = total + step_total(
        own,
        own_ids,
        jnp.where(odd, across_held, swapped_held),
        jnp.where(odd, across_ids, swapped_ids),
        my_pairs[1],
        False,
    )
    total = total + step_total(own, own_ids, fwd2_held, fwd2_ids, my_pairs[2], False)
    last = step_total(
        jnp.where(odd, own, back2_held),
        jnp.where(odd, own_ids, back2_ids),
        swapped_held,
        swapped_ids,
        jnp.where(odd, my_pairs[3], ahead_pairs[3]),
        False,
    )
    total = total + jnp.where(odd, last, 0.0)
    forward_part = jnp.where(odd, 0.0, last)
    totals = jnp.stack([total.reshape(device_count, capacity), forward_part.reshape(device_count, capacity)], axis=1)
    returned = lax.all_to_all(totals, "blk", split_axis=0, concat_axis=0, tiled=True)
    owner_sum = jnp.sum(
        jnp.where(place[:, None] == slot_index[None, :], returned[:, 0].reshape(-1)[None, :], 0.0), axis=1
    )
    behind = jnp.asarray(np.asarray(pos2dev, np.int32))[(owners - 2) % device_count] * capacity + arrival
    behind = jnp.where(owners % 2 == 0, behind, -1)
    handed_sum = jnp.sum(
        jnp.where(behind[:, None] == slot_index[None, :], returned[:, 1].reshape(-1)[None, :], 0.0), axis=1
    )
    return jnp.log1p(owner_sum + handed_sum)


def solution(mesh):
    placed = (
        P(("groups", "blk"), None),
        P(("groups", "blk")),
        P(("groups", "blk")),
        P(("groups", "blk"), None, None, None),
    )
    return jax.shard_map(
        body, mesh=mesh, in_specs=placed, out_specs=P(("groups", "blk")), check_vma=False
    )
```

```python
import numpy as np
import jax
import jax.numpy as jnp
from jax import lax
from jax.sharding import PartitionSpec as P

SLOTS = 1024
STEPS = 4


SHARPNESS_KNOB = 32.0


def ring_order(n):
    if n == 16:
        chips = [(z, 0) for z in range(4)] + [(z, 1) for z in reversed(range(4))]
        return [chips[p // 2][0] * 4 + chips[p // 2][1] * 2 + p % 2 for p in range(n)]
    return list(range(n))


def moved(x, pos2dev, moves):
    return lax.ppermute(x, "blk", [(pos2dev[a], pos2dev[b]) for a, b in moves])


def step_total(local, local_ids, remote, remote_ids, step_pairs, first_step):
    slot_count, feature_span = local.shape
    block_count = slot_count // 128
    logits = lax.dot_general(
        local, remote, (((1,), (1,)), ((), ())), preferred_element_type=jnp.float32
    ) * (SHARPNESS_KNOB / feature_span)
    keep = (local_ids[:, None] == remote_ids[None, :]) & (local_ids[:, None] >= 0)
    if first_step:
        keep = keep & jnp.logical_not(jnp.eye(slot_count, dtype=bool))
    contrib = jnp.where(keep, jnp.exp(logits), 0.0)
    per_block = contrib.reshape(slot_count, block_count, 128).sum(axis=2)
    counts = jnp.sum(
        step_pairs[:, :, None] == jnp.arange(block_count, dtype=jnp.int32), axis=1
    ).astype(jnp.float32)
    per_block = per_block.reshape(block_count, 128, block_count)
    return jnp.sum(per_block * counts[:, None, :], axis=2)


def unpack(packed, capacity):
    chunks = packed.reshape(-1, capacity + 1, packed.shape[-1])
    held = chunks[:, :capacity].reshape(-1, packed.shape[-1])
    return held, chunks[:, capacity, :capacity].reshape(-1).astype(jnp.int32)


def body(embeddings, owners, clusters, pairs):
    device_count = lax.axis_size("blk")
    row_count, feature_span = embeddings.shape
    slot_count = SLOTS
    capacity = slot_count // device_count
    block_count = slot_count // 128
    pos2dev = ring_order(device_count)
    dev2pos = np.argsort(np.asarray(pos2dev)).astype(np.int32)
    position = jnp.asarray(dev2pos)[lax.axis_index("blk")]
    odd = (position % 2) == 1

    value_entries = embeddings.astype(jnp.float32)
    unit = (
        value_entries
        * lax.rsqrt(jnp.mean(value_entries * value_entries, axis=1, keepdims=True) + 1e-06)
    ).astype(jnp.bfloat16)
    row_index = jnp.arange(row_count, dtype=jnp.int32)
    earlier = (owners[None, :] == owners[:, None]) & (row_index[None, :] < row_index[:, None])
    arrival = jnp.sum(earlier.astype(jnp.int32), axis=1)
    place = jnp.asarray(np.asarray(pos2dev, np.int32))[owners] * capacity + arrival
    slot_index = jnp.arange(slot_count, dtype=jnp.int32)
    hit = place[None, :] == slot_index[:, None]
    outgoing = jnp.dot(
        hit.astype(jnp.bfloat16), unit, preferred_element_type=jnp.float32
    ).astype(jnp.bfloat16)
    outgoing_ids = jnp.sum(jnp.where(hit, clusters[None, :] + 1, 0), axis=1) - 1
    pair_count = pairs[0].size
    side = jnp.concatenate(
        [
            outgoing_ids.reshape(device_count, capacity),
            jnp.broadcast_to(pairs[0].reshape(1, pair_count), (device_count, pair_count)),
        ],
        axis=1,
    ).astype(jnp.bfloat16)
    id_row = jnp.pad(side, ((0, 0), (0, feature_span - capacity - pair_count)))[:, None, :]
    payload = jnp.concatenate([outgoing.reshape(device_count, capacity, feature_span), id_row], axis=1)
    arrived = lax.all_to_all(payload, "blk", split_axis=0, concat_axis=0, tiled=True)
    all_pairs = (
        arrived[:, capacity, capacity : capacity + pair_count].astype(jnp.int32).reshape((device_count,) + pairs.shape[1:])
    )
    my_pairs = all_pairs[position]
    ahead_pairs = all_pairs[(position + 2) % device_count]

    n = device_count
    evens = range(0, n, 2)
    fwd2 = moved(arrived, pos2dev, [(p, (p + 2) % n) for p in range(n)])
    back2 = moved(arrived, pos2dev, [(p, (p - 2) % n) for p in evens])
    across = moved(arrived, pos2dev, [(p, p + 1) for p in evens])
    own, own_ids = unpack(arrived, capacity)
    total = step_total(own, own_ids, own, own_ids, my_pairs[0], True)
    total, back2, fwd2, across = lax.optimization_barrier((total, back2, fwd2, across))
    fwd2_swapped = moved(fwd2, pos2dev, [(p, p ^ 1) for p in range(n)])
    back2_held, back2_ids = unpack(back2, capacity)
    fwd2_held, fwd2_ids = unpack(fwd2, capacity)
    across_held, across_ids = unpack(across, capacity)
    swapped_held, swapped_ids = unpack(fwd2_swapped, capacity)

    total = total + step_total(
        own,
        own_ids,
        jnp.where(odd, across_held, swapped_held),
        jnp.where(odd, across_ids, swapped_ids),
        my_pairs[1],
        False,
    )
    total = total + step_total(own, own_ids, fwd2_held, fwd2_ids, my_pairs[2], False)
    last = step_total(
        jnp.where(odd, own, back2_held),
        jnp.where(odd, own_ids, back2_ids),
        swapped_held,
        swapped_ids,
        jnp.where(odd, my_pairs[3], ahead_pairs[3]),
        False,
    )
    total = total + jnp.where(odd, last, 0.0)
    forward_part = jnp.where(odd, 0.0, last)
    totals = jnp.stack([total.reshape(device_count, capacity), forward_part.reshape(device_count, capacity)], axis=1)
    returned = lax.all_to_all(totals, "blk", split_axis=0, concat_axis=0, tiled=True)
    owner_sum = jnp.sum(
        jnp.where(place[:, None] == slot_index[None, :], returned[:, 0].reshape(-1)[None, :], 0.0), axis=1
    )
    behind = jnp.asarray(np.asarray(pos2dev, np.int32))[(owners - 2) % device_count] * capacity + arrival
    behind = jnp.where(owners % 2 == 0, behind, -1)
    handed_sum = jnp.sum(
        jnp.where(behind[:, None] == slot_index[None, :], returned[:, 1].reshape(-1)[None, :], 0.0), axis=1
    )
    return jnp.log1p(owner_sum + handed_sum)


def solution(mesh):
    placed = (
        P(("groups", "blk"), None),
        P(("groups", "blk")),
        P(("groups", "blk")),
        P(("groups", "blk"), None, None, None),
    )
    return jax.shard_map(
        body, mesh=mesh, in_specs=placed, out_specs=P(("groups", "blk")), check_vma=False
    )
```

```python
import numpy as np
import jax
import jax.numpy as jnp
from jax import lax
from jax.sharding import PartitionSpec as P

SLOTS = 1024
STEPS = 4
ID_ROWS = 16


SHARPNESS_KNOB = 32.0


def ring_order(n):
    if n == 16:
        chips = [(z, 0) for z in range(4)] + [(z, 1) for z in reversed(range(4))]
        return [chips[p // 2][0] * 4 + chips[p // 2][1] * 2 + p % 2 for p in range(n)]
    return list(range(n))


def moved(x, pos2dev, moves):
    return lax.ppermute(x, "blk", [(pos2dev[a], pos2dev[b]) for a, b in moves])


def step_total(local, local_ids, remote, remote_ids, step_pairs, first_step):
    slot_count, feature_span = local.shape
    block_count = slot_count // 128
    logits = lax.dot_general(
        local, remote, (((1,), (1,)), ((), ())), preferred_element_type=jnp.float32
    ) * (SHARPNESS_KNOB / feature_span)
    keep = (local_ids[:, None] == remote_ids[None, :]) & (local_ids[:, None] >= 0)
    if first_step:
        keep = keep & jnp.logical_not(jnp.eye(slot_count, dtype=bool))
    contrib = jnp.where(keep, jnp.exp(logits), 0.0)
    per_block = contrib.reshape(slot_count, block_count, 128).sum(axis=2)
    counts = jnp.sum(
        step_pairs[:, :, None] == jnp.arange(block_count, dtype=jnp.int32), axis=1
    ).astype(jnp.float32)
    per_block = per_block.reshape(block_count, 128, block_count)
    return jnp.sum(per_block * counts[:, None, :], axis=2)


def pack(held, held_ids):
    feature_span = held.shape[1]
    id_rows = jnp.pad(held_ids.astype(jnp.bfloat16), (0, ID_ROWS * feature_span - held_ids.shape[0]))
    return jnp.concatenate([held, id_rows.reshape(ID_ROWS, feature_span)], axis=0)


def unpack(packed):
    slot_count = packed.shape[0] - ID_ROWS
    return packed[:slot_count], packed[slot_count:].reshape(-1)[:slot_count].astype(jnp.int32)


def body(embeddings, owners, clusters, pairs):
    device_count = lax.axis_size("blk")
    row_count, feature_span = embeddings.shape
    slot_count = SLOTS
    capacity = slot_count // device_count
    block_count = slot_count // 128
    pos2dev = ring_order(device_count)
    dev2pos = np.argsort(np.asarray(pos2dev)).astype(np.int32)
    position = jnp.asarray(dev2pos)[lax.axis_index("blk")]
    odd = (position % 2) == 1

    value_entries = embeddings.astype(jnp.float32)
    unit = (
        value_entries
        * lax.rsqrt(jnp.mean(value_entries * value_entries, axis=1, keepdims=True) + 1e-06)
    ).astype(jnp.bfloat16)
    row_index = jnp.arange(row_count, dtype=jnp.int32)
    earlier = (owners[None, :] == owners[:, None]) & (row_index[None, :] < row_index[:, None])
    arrival = jnp.sum(earlier.astype(jnp.int32), axis=1)
    place = jnp.asarray(np.asarray(pos2dev, np.int32))[owners] * capacity + arrival
    slot_index = jnp.arange(slot_count, dtype=jnp.int32)
    hit = place[None, :] == slot_index[:, None]
    outgoing = jnp.dot(
        hit.astype(jnp.bfloat16), unit, preferred_element_type=jnp.float32
    ).astype(jnp.bfloat16)
    outgoing_ids = jnp.sum(jnp.where(hit, clusters[None, :] + 1, 0), axis=1) - 1
    pair_count = pairs[0].size
    side = jnp.concatenate(
        [
            outgoing_ids.reshape(device_count, capacity),
            jnp.broadcast_to(pairs[0].reshape(1, pair_count), (device_count, pair_count)),
        ],
        axis=1,
    ).astype(jnp.bfloat16)
    id_row = jnp.pad(side, ((0, 0), (0, feature_span - capacity - pair_count)))[:, None, :]
    payload = jnp.concatenate([outgoing.reshape(device_count, capacity, feature_span), id_row], axis=1)
    arrived = lax.all_to_all(payload, "blk", split_axis=0, concat_axis=0, tiled=True)
    own = arrived[:, :capacity].reshape(slot_count, feature_span)
    own_ids = arrived[:, capacity, :capacity].reshape(slot_count).astype(jnp.int32)

    all_pairs = (
        arrived[:, capacity, capacity : capacity + pair_count].astype(jnp.int32).reshape((device_count,) + pairs.shape[1:])
    )
    my_pairs = all_pairs[position]
    ahead_pairs = all_pairs[(position + 2) % device_count]

    n = device_count
    evens = range(0, n, 2)
    packed = pack(own, own_ids)
    back2 = moved(packed, pos2dev, [(p, (p - 2) % n) for p in evens])
    fwd2 = moved(packed, pos2dev, [(p, (p + 2) % n) for p in range(n)])
    across = moved(packed, pos2dev, [(p, p + 1) for p in evens])
    total = step_total(own, own_ids, own, own_ids, my_pairs[0], True)
    total, back2, fwd2, across = lax.optimization_barrier((total, back2, fwd2, across))
    fwd2_swapped = moved(fwd2, pos2dev, [(p, p ^ 1) for p in range(n)])
    back2_held, back2_ids = unpack(back2)
    fwd2_held, fwd2_ids = unpack(fwd2)
    across_held, across_ids = unpack(across)
    swapped_held, swapped_ids = unpack(fwd2_swapped)

    total = total + step_total(
        own,
        own_ids,
        jnp.where(odd, across_held, swapped_held),
        jnp.where(odd, across_ids, swapped_ids),
        my_pairs[1],
        False,
    )
    total = total + step_total(own, own_ids, fwd2_held, fwd2_ids, my_pairs[2], False)
    last = step_total(
        jnp.where(odd, own, back2_held),
        jnp.where(odd, own_ids, back2_ids),
        swapped_held,
        swapped_ids,
        jnp.where(odd, my_pairs[3], ahead_pairs[3]),
        False,
    )
    total = total + jnp.where(odd, last, 0.0)
    forward_part = jnp.where(odd, 0.0, last)
    totals = jnp.stack([total.reshape(device_count, capacity), forward_part.reshape(device_count, capacity)], axis=1)
    gathered = lax.all_gather(totals, "blk", axis=0, tiled=False)
    returned = gathered[:, lax.axis_index("blk")]
    owner_sum = jnp.sum(
        jnp.where(place[:, None] == slot_index[None, :], returned[:, 0].reshape(-1)[None, :], 0.0), axis=1
    )
    behind = jnp.asarray(np.asarray(pos2dev, np.int32))[(owners - 2) % device_count] * capacity + arrival
    behind = jnp.where(owners % 2 == 0, behind, -1)
    handed_sum = jnp.sum(
        jnp.where(behind[:, None] == slot_index[None, :], returned[:, 1].reshape(-1)[None, :], 0.0), axis=1
    )
    return jnp.log1p(owner_sum + handed_sum)


def solution(mesh):
    placed = (
        P(("groups", "blk"), None),
        P(("groups", "blk")),
        P(("groups", "blk")),
        P(("groups", "blk"), None, None, None),
    )
    return jax.shard_map(
        body, mesh=mesh, in_specs=placed, out_specs=P(("groups", "blk")), check_vma=False
    )
```

```python
import numpy as np
import jax
import jax.numpy as jnp
from jax import lax
from jax.sharding import PartitionSpec as P

SLOTS = 1024
STEPS = 4
ID_ROWS = 16


SHARPNESS_KNOB = 32.0


def ring_order(n):
    if n == 16:
        chips = [(z, 0) for z in range(4)] + [(z, 1) for z in reversed(range(4))]
        return [chips[p // 2][0] * 4 + chips[p // 2][1] * 2 + p % 2 for p in range(n)]
    return list(range(n))


def moved(x, pos2dev, moves):
    return lax.ppermute(x, "blk", [(pos2dev[a], pos2dev[b]) for a, b in moves])


def step_total(local, local_ids, remote, remote_ids, step_pairs, first_step, first_block=0):
    slot_count, feature_span = local.shape
    block_count = slot_count // 128
    remote_blocks = remote.shape[0] // 128
    logits = lax.dot_general(
        local, remote, (((1,), (1,)), ((), ())), preferred_element_type=jnp.float32
    ) * (SHARPNESS_KNOB / feature_span)
    keep = (local_ids[:, None] == remote_ids[None, :]) & (local_ids[:, None] >= 0)
    if first_step:
        keep = keep & jnp.logical_not(jnp.eye(slot_count, dtype=bool))
    contrib = jnp.where(keep, jnp.exp(logits), 0.0)
    per_block = contrib.reshape(slot_count, remote_blocks, 128).sum(axis=2)
    named = first_block + jnp.arange(remote_blocks, dtype=jnp.int32)
    counts = jnp.sum(step_pairs[:, :, None] == named, axis=1).astype(jnp.float32)
    per_block = per_block.reshape(block_count, 128, remote_blocks)
    return jnp.sum(per_block * counts[:, None, :], axis=2)


def pack(held, held_ids):
    feature_span = held.shape[1]
    id_rows = jnp.pad(held_ids.astype(jnp.bfloat16), (0, ID_ROWS * feature_span - held_ids.shape[0]))
    return jnp.concatenate([held, id_rows.reshape(ID_ROWS, feature_span)], axis=0)


def unpack(packed):
    slot_count = packed.shape[0] - ID_ROWS
    return packed[:slot_count], packed[slot_count:].reshape(-1)[:slot_count].astype(jnp.int32)


def body(embeddings, owners, clusters, pairs):
    device_count = lax.axis_size("blk")
    row_count, feature_span = embeddings.shape
    slot_count = SLOTS
    capacity = slot_count // device_count
    block_count = slot_count // 128
    pos2dev = ring_order(device_count)
    dev2pos = np.argsort(np.asarray(pos2dev)).astype(np.int32)
    position = jnp.asarray(dev2pos)[lax.axis_index("blk")]
    odd = (position % 2) == 1

    value_entries = embeddings.astype(jnp.float32)
    unit = (
        value_entries
        * lax.rsqrt(jnp.mean(value_entries * value_entries, axis=1, keepdims=True) + 1e-06)
    ).astype(jnp.bfloat16)
    row_index = jnp.arange(row_count, dtype=jnp.int32)
    earlier = (owners[None, :] == owners[:, None]) & (row_index[None, :] < row_index[:, None])
    arrival = jnp.sum(earlier.astype(jnp.int32), axis=1)
    place = jnp.asarray(np.asarray(pos2dev, np.int32))[owners] * capacity + arrival
    slot_index = jnp.arange(slot_count, dtype=jnp.int32)
    hit = place[None, :] == slot_index[:, None]
    outgoing = jnp.dot(
        hit.astype(jnp.bfloat16), unit, preferred_element_type=jnp.float32
    ).astype(jnp.bfloat16)
    outgoing_ids = jnp.sum(jnp.where(hit, clusters[None, :] + 1, 0), axis=1) - 1
    pair_count = pairs[0].size
    side = jnp.concatenate(
        [
            outgoing_ids.reshape(device_count, capacity),
            jnp.broadcast_to(pairs[0].reshape(1, pair_count), (device_count, pair_count)),
        ],
        axis=1,
    ).astype(jnp.bfloat16)
    id_row = jnp.pad(side, ((0, 0), (0, feature_span - capacity - pair_count)))[:, None, :]
    payload = jnp.concatenate([outgoing.reshape(device_count, capacity, feature_span), id_row], axis=1)
    arrived = lax.all_to_all(payload, "blk", split_axis=0, concat_axis=0, tiled=True)
    own = arrived[:, :capacity].reshape(slot_count, feature_span)
    own_ids = arrived[:, capacity, :capacity].reshape(slot_count).astype(jnp.int32)

    all_pairs = (
        arrived[:, capacity, capacity : capacity + pair_count].astype(jnp.int32).reshape((device_count,) + pairs.shape[1:])
    )
    my_pairs = all_pairs[position]
    ahead_pairs = all_pairs[(position + 2) % device_count]

    n = device_count
    evens = range(0, n, 2)
    half = slot_count // 2
    half_blocks = block_count // 2
    packed = pack(own, own_ids)
    first_half = pack(own[:half], own_ids[:half])
    back2 = moved(packed, pos2dev, [(p, (p - 2) % n) for p in evens])
    fwd_a = moved(first_half, pos2dev, [(p, (p + 2) % n) for p in range(n)])
    across = moved(packed, pos2dev, [(p, p + 1) for p in evens])
    total = step_total(own, own_ids, own, own_ids, my_pairs[0], True)
    total, fwd_a, across, back2 = lax.optimization_barrier((total, fwd_a, across, back2))
    _, second_half = lax.optimization_barrier((fwd_a, pack(own[half:], own_ids[half:])))
    fwd_b = moved(second_half, pos2dev, [(p, (p + 2) % n) for p in range(n)])
    across_held, across_ids = unpack(across)
    swap = [(p, p ^ 1) for p in range(n)]
    last = 0.0
    fwd = fwd_a
    for lo in (0, half):
        if lo:
            fwd, total, last = lax.optimization_barrier((fwd_b, total, last))
        swapped_held, swapped_ids = unpack(moved(fwd, pos2dev, swap))
        fwd_held, fwd_ids = unpack(fwd)
        q0 = lo // 128
        total = total + step_total(own, own_ids, fwd_held, fwd_ids, my_pairs[2], False, q0)
        total = total + step_total(
            own,
            own_ids,
            jnp.where(odd, across_held[lo : lo + half], swapped_held),
            jnp.where(odd, across_ids[lo : lo + half], swapped_ids),
            my_pairs[1],
            False,
            q0,
        )
        back2_held, back2_ids = unpack(back2)
        last = last + step_total(
            jnp.where(odd, own, back2_held),
            jnp.where(odd, own_ids, back2_ids),
            swapped_held,
            swapped_ids,
            jnp.where(odd, my_pairs[3], ahead_pairs[3]),
            False,
            q0,
        )
    total = total + jnp.where(odd, last, 0.0)
    forward_part = jnp.where(odd, 0.0, last)
    totals = jnp.stack([total.reshape(device_count, capacity), forward_part.reshape(device_count, capacity)], axis=1)
    returned = lax.all_to_all(totals, "blk", split_axis=0, concat_axis=0, tiled=True)
    owner_sum = jnp.sum(
        jnp.where(place[:, None] == slot_index[None, :], returned[:, 0].reshape(-1)[None, :], 0.0), axis=1
    )
    behind = jnp.asarray(np.asarray(pos2dev, np.int32))[(owners - 2) % device_count] * capacity + arrival
    behind = jnp.where(owners % 2 == 0, behind, -1)
    handed_sum = jnp.sum(
        jnp.where(behind[:, None] == slot_index[None, :], returned[:, 1].reshape(-1)[None, :], 0.0), axis=1
    )
    return jnp.log1p(owner_sum + handed_sum)


def solution(mesh):
    placed = (
        P(("groups", "blk"), None),
        P(("groups", "blk")),
        P(("groups", "blk")),
        P(("groups", "blk"), None, None, None),
    )
    return jax.shard_map(
        body, mesh=mesh, in_specs=placed, out_specs=P(("groups", "blk")), check_vma=False
    )
```

```python
import numpy as np
import jax
import jax.numpy as jnp
from jax import lax
from jax.sharding import PartitionSpec as P

SLOTS = 1024
STEPS = 4
ID_ROWS = 16


SHARPNESS_KNOB = 32.0


def ring_order(n):
    if n == 16:
        chips = [(z, 0) for z in range(4)] + [(z, 1) for z in reversed(range(4))]
        return [chips[p // 2][0] * 4 + chips[p // 2][1] * 2 + p % 2 for p in range(n)]
    return list(range(n))


def moved(x, pos2dev, moves):
    return lax.ppermute(x, "blk", [(pos2dev[a], pos2dev[b]) for a, b in moves])


def step_total(local, local_ids, remote, remote_ids, step_pairs, first_step, first_block=0):
    slot_count, feature_span = local.shape
    block_count = slot_count // 128
    remote_blocks = remote.shape[0] // 128
    logits = lax.dot_general(
        local, remote, (((1,), (1,)), ((), ())), preferred_element_type=jnp.float32
    ) * (SHARPNESS_KNOB / feature_span)
    keep = (local_ids[:, None] == remote_ids[None, :]) & (local_ids[:, None] >= 0)
    if first_step:
        keep = keep & jnp.logical_not(jnp.eye(slot_count, dtype=bool))
    contrib = jnp.where(keep, jnp.exp(logits), 0.0)
    per_block = contrib.reshape(slot_count, remote_blocks, 128).sum(axis=2)
    named = first_block + jnp.arange(remote_blocks, dtype=jnp.int32)
    counts = jnp.sum(step_pairs[:, :, None] == named, axis=1).astype(jnp.float32)
    per_block = per_block.reshape(block_count, 128, remote_blocks)
    return jnp.sum(per_block * counts[:, None, :], axis=2)


def pack(held, held_ids):
    feature_span = held.shape[1]
    id_rows = jnp.pad(held_ids.astype(jnp.bfloat16), (0, ID_ROWS * feature_span - held_ids.shape[0]))
    return jnp.concatenate([held, id_rows.reshape(ID_ROWS, feature_span)], axis=0)


def unpack(packed):
    slot_count = packed.shape[0] - ID_ROWS
    return packed[:slot_count], packed[slot_count:].reshape(-1)[:slot_count].astype(jnp.int32)


def body(embeddings, owners, clusters, pairs):
    device_count = lax.axis_size("blk")
    row_count, feature_span = embeddings.shape
    slot_count = SLOTS
    capacity = slot_count // device_count
    block_count = slot_count // 128
    pos2dev = ring_order(device_count)
    dev2pos = np.argsort(np.asarray(pos2dev)).astype(np.int32)
    position = jnp.asarray(dev2pos)[lax.axis_index("blk")]
    odd = (position % 2) == 1

    value_entries = embeddings.astype(jnp.float32)
    unit = (
        value_entries
        * lax.rsqrt(jnp.mean(value_entries * value_entries, axis=1, keepdims=True) + 1e-06)
    ).astype(jnp.bfloat16)
    row_index = jnp.arange(row_count, dtype=jnp.int32)
    earlier = (owners[None, :] == owners[:, None]) & (row_index[None, :] < row_index[:, None])
    arrival = jnp.sum(earlier.astype(jnp.int32), axis=1)
    place = jnp.asarray(np.asarray(pos2dev, np.int32))[owners] * capacity + arrival
    slot_index = jnp.arange(slot_count, dtype=jnp.int32)
    hit = place[None, :] == slot_index[:, None]
    outgoing = jnp.dot(
        hit.astype(jnp.bfloat16), unit, preferred_element_type=jnp.float32
    ).astype(jnp.bfloat16)
    outgoing_ids = jnp.sum(jnp.where(hit, clusters[None, :] + 1, 0), axis=1) - 1
    pair_count = pairs[0].size
    side = jnp.concatenate(
        [
            outgoing_ids.reshape(device_count, capacity),
            jnp.broadcast_to(pairs[0].reshape(1, pair_count), (device_count, pair_count)),
        ],
        axis=1,
    ).astype(jnp.bfloat16)
    id_row = jnp.pad(side, ((0, 0), (0, feature_span - capacity - pair_count)))[:, None, :]
    payload = jnp.concatenate([outgoing.reshape(device_count, capacity, feature_span), id_row], axis=1)
    arrived = lax.all_to_all(payload, "blk", split_axis=0, concat_axis=0, tiled=True)
    own = arrived[:, :capacity].reshape(slot_count, feature_span)
    own_ids = arrived[:, capacity, :capacity].reshape(slot_count).astype(jnp.int32)

    all_pairs = (
        arrived[:, capacity, capacity : capacity + pair_count].astype(jnp.int32).reshape((device_count,) + pairs.shape[1:])
    )
    my_pairs = all_pairs[position]
    ahead_pairs = all_pairs[(position + 2) % device_count]

    n = device_count
    evens = range(0, n, 2)
    half = slot_count // 2
    forward = [(p, (p + 2) % n) for p in range(n)]
    swap = [(p, p ^ 1) for p in range(n)]
    fwd_a = moved(pack(own[:half], own_ids[:half]), pos2dev, forward)
    total = step_total(own, own_ids, own, own_ids, my_pairs[0], True)
    total, fwd_a = lax.optimization_barrier((total, fwd_a))
    _, second_half, packed = lax.optimization_barrier(
        (fwd_a, pack(own[half:], own_ids[half:]), pack(own, own_ids))
    )
    fwd_b = moved(second_half, pos2dev, forward)
    back2 = moved(packed, pos2dev, [(p, (p - 2) % n) for p in evens])
    across = moved(packed, pos2dev, [(p, p + 1) for p in evens])
    swapped_a = moved(fwd_a, pos2dev, swap)
    across_held, across_ids = unpack(across)

    def half_steps(fwd, swapped, lo, total):
        fwd_held, fwd_ids = unpack(fwd)
        swapped_held, swapped_ids = unpack(swapped)
        q0 = lo // 128
        total = total + step_total(own, own_ids, fwd_held, fwd_ids, my_pairs[2], False, q0)
        return total + step_total(
            own,
            own_ids,
            jnp.where(odd, across_held[lo : lo + half], swapped_held),
            jnp.where(odd, across_ids[lo : lo + half], swapped_ids),
            my_pairs[1],
            False,
            q0,
        )

    def last_step(swapped, lo):
        back2_held, back2_ids = unpack(back2)
        swapped_held, swapped_ids = unpack(swapped)
        return step_total(
            jnp.where(odd, own, back2_held),
            jnp.where(odd, own_ids, back2_ids),
            swapped_held,
            swapped_ids,
            jnp.where(odd, my_pairs[3], ahead_pairs[3]),
            False,
            lo // 128,
        )

    total = half_steps(fwd_a, swapped_a, 0, total)
    fwd_b, total = lax.optimization_barrier((fwd_b, total))
    swapped_b = moved(fwd_b, pos2dev, swap)
    total = half_steps(fwd_b, swapped_b, half, total)
    last = last_step(swapped_a, 0) + last_step(swapped_b, half)
    total = total + jnp.where(odd, last, 0.0)
    forward_part = jnp.where(odd, 0.0, last)
    totals = jnp.stack([total.reshape(device_count, capacity), forward_part.reshape(device_count, capacity)], axis=1)
    returned = lax.all_to_all(totals, "blk", split_axis=0, concat_axis=0, tiled=True)
    owner_sum = jnp.sum(
        jnp.where(place[:, None] == slot_index[None, :], returned[:, 0].reshape(-1)[None, :], 0.0), axis=1
    )
    behind = jnp.asarray(np.asarray(pos2dev, np.int32))[(owners - 2) % device_count] * capacity + arrival
    behind = jnp.where(owners % 2 == 0, behind, -1)
    handed_sum = jnp.sum(
        jnp.where(behind[:, None] == slot_index[None, :], returned[:, 1].reshape(-1)[None, :], 0.0), axis=1
    )
    return jnp.log1p(owner_sum + handed_sum)


def solution(mesh):
    placed = (
        P(("groups", "blk"), None),
        P(("groups", "blk")),
        P(("groups", "blk")),
        P(("groups", "blk"), None, None, None),
    )
    return jax.shard_map(
        body, mesh=mesh, in_specs=placed, out_specs=P(("groups", "blk")), check_vma=False
    )
```

```python
import numpy as np
import jax
import jax.numpy as jnp
from jax import lax
from jax.sharding import PartitionSpec as P

SLOTS = 1024
STEPS = 4
ID_ROWS = 16


SHARPNESS_KNOB = 32.0


def ring_order(n):
    if n == 16:
        chips = [(z, 0) for z in range(4)] + [(z, 1) for z in reversed(range(4))]
        return [chips[p // 2][0] * 4 + chips[p // 2][1] * 2 + p % 2 for p in range(n)]
    return list(range(n))


def moved(x, pos2dev, moves):
    return lax.ppermute(x, "blk", [(pos2dev[a], pos2dev[b]) for a, b in moves])


def step_total(local, local_ids, remote, remote_ids, step_pairs, first_step, first_block=0):
    slot_count, feature_span = local.shape
    block_count = slot_count // 128
    remote_blocks = remote.shape[0] // 128
    logits = lax.dot_general(
        local, remote, (((1,), (1,)), ((), ())), preferred_element_type=jnp.float32
    ) * (SHARPNESS_KNOB / feature_span)
    keep = (local_ids[:, None] == remote_ids[None, :]) & (local_ids[:, None] >= 0)
    if first_step:
        keep = keep & jnp.logical_not(jnp.eye(slot_count, dtype=bool))
    contrib = jnp.where(keep, jnp.exp(logits), 0.0)
    per_block = contrib.reshape(slot_count, remote_blocks, 128).sum(axis=2)
    named = first_block + jnp.arange(remote_blocks, dtype=jnp.int32)
    counts = jnp.sum(step_pairs[:, :, None] == named, axis=1).astype(jnp.float32)
    per_block = per_block.reshape(block_count, 128, remote_blocks)
    return jnp.sum(per_block * counts[:, None, :], axis=2)


def pack(held, held_ids):
    feature_span = held.shape[1]
    id_rows = jnp.pad(held_ids.astype(jnp.bfloat16), (0, ID_ROWS * feature_span - held_ids.shape[0]))
    return jnp.concatenate([held, id_rows.reshape(ID_ROWS, feature_span)], axis=0)


def unpack(packed):
    slot_count = packed.shape[0] - ID_ROWS
    return packed[:slot_count], packed[slot_count:].reshape(-1)[:slot_count].astype(jnp.int32)


def body(embeddings, owners, clusters, pairs):
    device_count = lax.axis_size("blk")
    row_count, feature_span = embeddings.shape
    slot_count = SLOTS
    capacity = slot_count // device_count
    block_count = slot_count // 128
    pos2dev = ring_order(device_count)
    dev2pos = np.argsort(np.asarray(pos2dev)).astype(np.int32)
    position = jnp.asarray(dev2pos)[lax.axis_index("blk")]
    odd = (position % 2) == 1

    value_entries = embeddings.astype(jnp.float32)
    unit = (
        value_entries
        * lax.rsqrt(jnp.mean(value_entries * value_entries, axis=1, keepdims=True) + 1e-06)
    ).astype(jnp.bfloat16)
    row_index = jnp.arange(row_count, dtype=jnp.int32)
    earlier = (owners[None, :] == owners[:, None]) & (row_index[None, :] < row_index[:, None])
    arrival = jnp.sum(earlier.astype(jnp.int32), axis=1)
    place = jnp.asarray(np.asarray(pos2dev, np.int32))[owners] * capacity + arrival
    slot_index = jnp.arange(slot_count, dtype=jnp.int32)
    hit = place[None, :] == slot_index[:, None]
    outgoing = jnp.dot(
        hit.astype(jnp.bfloat16), unit, preferred_element_type=jnp.float32
    ).astype(jnp.bfloat16)
    outgoing_ids = jnp.sum(jnp.where(hit, clusters[None, :] + 1, 0), axis=1) - 1
    pair_count = pairs[0].size
    side = jnp.concatenate(
        [
            outgoing_ids.reshape(device_count, capacity),
            jnp.broadcast_to(pairs[0].reshape(1, pair_count), (device_count, pair_count)),
        ],
        axis=1,
    ).astype(jnp.bfloat16)
    id_row = jnp.pad(side, ((0, 0), (0, feature_span - capacity - pair_count)))[:, None, :]
    payload = jnp.concatenate([outgoing.reshape(device_count, capacity, feature_span), id_row], axis=1)
    arrived = lax.all_to_all(payload, "blk", split_axis=0, concat_axis=0, tiled=True)
    own = arrived[:, :capacity].reshape(slot_count, feature_span)
    own_ids = arrived[:, capacity, :capacity].reshape(slot_count).astype(jnp.int32)

    all_pairs = (
        arrived[:, capacity, capacity : capacity + pair_count].astype(jnp.int32).reshape((device_count,) + pairs.shape[1:])
    )
    my_pairs = all_pairs[position]
    ahead_pairs = all_pairs[(position + 2) % device_count]

    n = device_count
    evens = range(0, n, 2)
    half = slot_count // 2
    forward = [(p, (p + 2) % n) for p in range(n)]
    swap = [(p, p ^ 1) for p in range(n)]
    fwd_a = moved(pack(own[:half], own_ids[:half]), pos2dev, forward)
    across = moved(pack(own, own_ids), pos2dev, [(p, p + 1) for p in evens])
    total = step_total(own, own_ids, own, own_ids, my_pairs[0], True)
    total, fwd_a, across = lax.optimization_barrier((total, fwd_a, across))
    _, second_half, packed = lax.optimization_barrier(
        (fwd_a, pack(own[half:], own_ids[half:]), pack(own, own_ids))
    )
    fwd_b = moved(second_half, pos2dev, forward)
    back2 = moved(packed, pos2dev, [(p, (p - 2) % n) for p in evens])
    swapped_a = moved(fwd_a, pos2dev, swap)
    across_held, across_ids = unpack(across)

    def half_steps(fwd, swapped, lo, total):
        fwd_held, fwd_ids = unpack(fwd)
        swapped_held, swapped_ids = unpack(swapped)
        q0 = lo // 128
        total = total + step_total(own, own_ids, fwd_held, fwd_ids, my_pairs[2], False, q0)
        return total + step_total(
            own,
            own_ids,
            jnp.where(odd, across_held[lo : lo + half], swapped_held),
            jnp.where(odd, across_ids[lo : lo + half], swapped_ids),
            my_pairs[1],
            False,
            q0,
        )

    def last_step(swapped, lo):
        back2_held, back2_ids = unpack(back2)
        swapped_held, swapped_ids = unpack(swapped)
        return step_total(
            jnp.where(odd, own, back2_held),
            jnp.where(odd, own_ids, back2_ids),
            swapped_held,
            swapped_ids,
            jnp.where(odd, my_pairs[3], ahead_pairs[3]),
            False,
            lo // 128,
        )

    total = half_steps(fwd_a, swapped_a, 0, total)
    fwd_b, total = lax.optimization_barrier((fwd_b, total))
    swapped_b = moved(fwd_b, pos2dev, swap)
    total = half_steps(fwd_b, swapped_b, half, total)
    last = last_step(swapped_a, 0) + last_step(swapped_b, half)
    total = total + jnp.where(odd, last, 0.0)
    forward_part = jnp.where(odd, 0.0, last)
    totals = jnp.stack([total.reshape(device_count, capacity), forward_part.reshape(device_count, capacity)], axis=1)
    returned = lax.all_to_all(totals, "blk", split_axis=0, concat_axis=0, tiled=True)
    owner_sum = jnp.sum(
        jnp.where(place[:, None] == slot_index[None, :], returned[:, 0].reshape(-1)[None, :], 0.0), axis=1
    )
    behind = jnp.asarray(np.asarray(pos2dev, np.int32))[(owners - 2) % device_count] * capacity + arrival
    behind = jnp.where(owners % 2 == 0, behind, -1)
    handed_sum = jnp.sum(
        jnp.where(behind[:, None] == slot_index[None, :], returned[:, 1].reshape(-1)[None, :], 0.0), axis=1
    )
    return jnp.log1p(owner_sum + handed_sum)


def solution(mesh):
    placed = (
        P(("groups", "blk"), None),
        P(("groups", "blk")),
        P(("groups", "blk")),
        P(("groups", "blk"), None, None, None),
    )
    return jax.shard_map(
        body, mesh=mesh, in_specs=placed, out_specs=P(("groups", "blk")), check_vma=False
    )
```

```python
import numpy as np
import jax
import jax.numpy as jnp
from jax import lax
from jax.sharding import PartitionSpec as P

SLOTS = 1024
STEPS = 4
ID_ROWS = 16


SHARPNESS_KNOB = 32.0


def ring_order(n):
    if n == 16:
        chips = [(z, 0) for z in range(4)] + [(z, 1) for z in reversed(range(4))]
        return [chips[p // 2][0] * 4 + chips[p // 2][1] * 2 + p % 2 for p in range(n)]
    return list(range(n))


def moved(x, pos2dev, moves):
    return lax.ppermute(x, "blk", [(pos2dev[a], pos2dev[b]) for a, b in moves])


def step_total(local, local_ids, remote, remote_ids, step_pairs, first_step, first_block=0):
    slot_count, feature_span = local.shape
    block_count = slot_count // 128
    remote_blocks = remote.shape[0] // 128
    logits = lax.dot_general(
        local, remote, (((1,), (1,)), ((), ())), preferred_element_type=jnp.float32
    ) * (SHARPNESS_KNOB / feature_span)
    keep = (local_ids[:, None] == remote_ids[None, :]) & (local_ids[:, None] >= 0)
    if first_step:
        keep = keep & jnp.logical_not(jnp.eye(slot_count, dtype=bool))
    contrib = jnp.where(keep, jnp.exp(logits), 0.0)
    per_block = contrib.reshape(slot_count, remote_blocks, 128).sum(axis=2)
    named = first_block + jnp.arange(remote_blocks, dtype=jnp.int32)
    counts = jnp.sum(step_pairs[:, :, None] == named, axis=1).astype(jnp.float32)
    per_block = per_block.reshape(block_count, 128, remote_blocks)
    return jnp.sum(per_block * counts[:, None, :], axis=2)


def pack(held, held_ids):
    feature_span = held.shape[1]
    id_rows = jnp.pad(held_ids.astype(jnp.bfloat16), (0, ID_ROWS * feature_span - held_ids.shape[0]))
    return jnp.concatenate([held, id_rows.reshape(ID_ROWS, feature_span)], axis=0)


def unpack(packed):
    slot_count = packed.shape[0] - ID_ROWS
    return packed[:slot_count], packed[slot_count:].reshape(-1)[:slot_count].astype(jnp.int32)


def body(embeddings, owners, clusters, pairs):
    device_count = lax.axis_size("blk")
    row_count, feature_span = embeddings.shape
    slot_count = SLOTS
    capacity = slot_count // device_count
    block_count = slot_count // 128
    pos2dev = ring_order(device_count)
    dev2pos = np.argsort(np.asarray(pos2dev)).astype(np.int32)
    position = jnp.asarray(dev2pos)[lax.axis_index("blk")]
    odd = (position % 2) == 1

    value_entries = embeddings.astype(jnp.float32)
    unit = (
        value_entries
        * lax.rsqrt(jnp.mean(value_entries * value_entries, axis=1, keepdims=True) + 1e-06)
    ).astype(jnp.bfloat16)
    row_index = jnp.arange(row_count, dtype=jnp.int32)
    earlier = (owners[None, :] == owners[:, None]) & (row_index[None, :] < row_index[:, None])
    arrival = jnp.sum(earlier.astype(jnp.int32), axis=1)
    place = jnp.asarray(np.asarray(pos2dev, np.int32))[owners] * capacity + arrival
    slot_index = jnp.arange(slot_count, dtype=jnp.int32)
    hit = place[None, :] == slot_index[:, None]
    outgoing = jnp.dot(
        hit.astype(jnp.bfloat16), unit, preferred_element_type=jnp.float32
    ).astype(jnp.bfloat16)
    outgoing_ids = jnp.sum(jnp.where(hit, clusters[None, :] + 1, 0), axis=1) - 1
    pair_count = pairs[0].size
    side = jnp.concatenate(
        [
            outgoing_ids.reshape(device_count, capacity),
            jnp.broadcast_to(pairs[0].reshape(1, pair_count), (device_count, pair_count)),
        ],
        axis=1,
    ).astype(jnp.bfloat16)
    id_row = jnp.pad(side, ((0, 0), (0, feature_span - capacity - pair_count)))[:, None, :]
    payload = jnp.concatenate([outgoing.reshape(device_count, capacity, feature_span), id_row], axis=1)
    arrived = lax.all_to_all(payload, "blk", split_axis=0, concat_axis=0, tiled=True)
    own = arrived[:, :capacity].reshape(slot_count, feature_span)
    own_ids = arrived[:, capacity, :capacity].reshape(slot_count).astype(jnp.int32)

    all_pairs = (
        arrived[:, capacity, capacity : capacity + pair_count].astype(jnp.int32).reshape((device_count,) + pairs.shape[1:])
    )
    my_pairs = all_pairs[position]
    ahead_pairs = all_pairs[(position + 2) % device_count]

    n = device_count
    evens = range(0, n, 2)
    half = slot_count // 2
    forward = [(p, (p + 2) % n) for p in range(n)]
    swap = [(p, p ^ 1) for p in range(n)]
    packed = pack(own, own_ids)
    packed = jnp.concatenate([packed[:half], packed[slot_count:], packed[half:slot_count]], axis=0)
    lead = half + packed.shape[0] - slot_count

    def ids_of(rows):
        return rows.reshape(-1)[:slot_count].astype(jnp.int32)

    fwd_a = moved(packed[:lead], pos2dev, forward)
    total = step_total(own, own_ids, own, own_ids, my_pairs[0], True)
    total, fwd_a = lax.optimization_barrier((total, fwd_a))
    _, second_half, late = lax.optimization_barrier((fwd_a, own[half:], packed))
    fwd_b = moved(second_half, pos2dev, forward)
    back2 = moved(late, pos2dev, [(p, (p - 2) % n) for p in evens])
    partner = moved(jnp.concatenate([fwd_a, late], axis=0), pos2dev, swap)
    swapped_a, across = partner[:lead], partner[lead:]
    across_ids = ids_of(across[half:lead])
    fwd_ids = ids_of(fwd_a[half:lead])

    def half_steps(fwd, swapped, swapped_ids, lo, total):
        q0 = lo // 128
        total = total + step_total(own, own_ids, fwd[:half], fwd_ids[lo : lo + half], my_pairs[2], False, q0)
        across_rows = across[:half] if lo == 0 else across[lead:]
        return total + step_total(
            own,
            own_ids,
            jnp.where(odd, across_rows, swapped[:half]),
            jnp.where(odd, across_ids[lo : lo + half], swapped_ids[lo : lo + half]),
            my_pairs[1],
            False,
            q0,
        )

    def last_step(swapped, swapped_ids, lo):
        back2_held = jnp.concatenate([back2[:half], back2[lead:]], axis=0)
        back2_ids = ids_of(back2[half:lead])
        return step_total(
            jnp.where(odd, own, back2_held),
            jnp.where(odd, own_ids, back2_ids),
            swapped[:half],
            swapped_ids[lo : lo + half],
            jnp.where(odd, my_pairs[3], ahead_pairs[3]),
            False,
            lo // 128,
        )

    swapped_ids = ids_of(swapped_a[half:lead])
    total = half_steps(fwd_a, swapped_a, swapped_ids, 0, total)
    fwd_b, total = lax.optimization_barrier((fwd_b, total))
    swapped_b = moved(fwd_b, pos2dev, swap)
    total = half_steps(fwd_b, swapped_b, swapped_ids, half, total)
    last = last_step(swapped_a, swapped_ids, 0) + last_step(swapped_b, swapped_ids, half)
    total = total + jnp.where(odd, last, 0.0)
    forward_part = jnp.where(odd, 0.0, last)
    totals = jnp.stack([total.reshape(device_count, capacity), forward_part.reshape(device_count, capacity)], axis=1)
    returned = lax.all_to_all(totals, "blk", split_axis=0, concat_axis=0, tiled=True)
    owner_sum = jnp.sum(
        jnp.where(place[:, None] == slot_index[None, :], returned[:, 0].reshape(-1)[None, :], 0.0), axis=1
    )
    behind = jnp.asarray(np.asarray(pos2dev, np.int32))[(owners - 2) % device_count] * capacity + arrival
    behind = jnp.where(owners % 2 == 0, behind, -1)
    handed_sum = jnp.sum(
        jnp.where(behind[:, None] == slot_index[None, :], returned[:, 1].reshape(-1)[None, :], 0.0), axis=1
    )
    return jnp.log1p(owner_sum + handed_sum)


def solution(mesh):
    placed = (
        P(("groups", "blk"), None),
        P(("groups", "blk")),
        P(("groups", "blk")),
        P(("groups", "blk"), None, None, None),
    )
    return jax.shard_map(
        body, mesh=mesh, in_specs=placed, out_specs=P(("groups", "blk")), check_vma=False
    )
```

```python
import numpy as np
import jax
import jax.numpy as jnp
from jax import lax
from jax.sharding import PartitionSpec as P

SLOTS = 1024
STEPS = 4
ID_ROWS = 16


SHARPNESS_KNOB = 32.0


def ring_order(n):
    if n == 16:
        chips = [(z, 0) for z in range(4)] + [(z, 1) for z in reversed(range(4))]
        return [chips[p // 2][0] * 4 + chips[p // 2][1] * 2 + p % 2 for p in range(n)]
    return list(range(n))


def moved(x, pos2dev, moves):
    return lax.ppermute(x, "blk", [(pos2dev[a], pos2dev[b]) for a, b in moves])


def step_total(local, local_ids, remote, remote_ids, step_pairs, first_step, first_block=0):
    slot_count, feature_span = local.shape
    block_count = slot_count // 128
    remote_blocks = remote.shape[0] // 128
    logits = lax.dot_general(
        local, remote, (((1,), (1,)), ((), ())), preferred_element_type=jnp.float32
    ) * (SHARPNESS_KNOB / feature_span)
    keep = (local_ids[:, None] == remote_ids[None, :]) & (local_ids[:, None] >= 0)
    if first_step:
        keep = keep & jnp.logical_not(jnp.eye(slot_count, dtype=bool))
    contrib = jnp.where(keep, jnp.exp(logits), 0.0)
    per_block = contrib.reshape(slot_count, remote_blocks, 128).sum(axis=2)
    named = first_block + jnp.arange(remote_blocks, dtype=jnp.int32)
    counts = jnp.sum(step_pairs[:, :, None] == named, axis=1).astype(jnp.float32)
    per_block = per_block.reshape(block_count, 128, remote_blocks)
    return jnp.sum(per_block * counts[:, None, :], axis=2)


def pack(held, held_ids):
    feature_span = held.shape[1]
    id_rows = jnp.pad(held_ids.astype(jnp.bfloat16), (0, ID_ROWS * feature_span - held_ids.shape[0]))
    return jnp.concatenate([held, id_rows.reshape(ID_ROWS, feature_span)], axis=0)


def unpack(packed):
    slot_count = packed.shape[0] - ID_ROWS
    return packed[:slot_count], packed[slot_count:].reshape(-1)[:slot_count].astype(jnp.int32)


def body(embeddings, owners, clusters, pairs):
    device_count = lax.axis_size("blk")
    row_count, feature_span = embeddings.shape
    slot_count = SLOTS
    capacity = slot_count // device_count
    block_count = slot_count // 128
    pos2dev = ring_order(device_count)
    dev2pos = np.argsort(np.asarray(pos2dev)).astype(np.int32)
    position = jnp.asarray(dev2pos)[lax.axis_index("blk")]
    odd = (position % 2) == 1

    value_entries = embeddings.astype(jnp.float32)
    unit = (
        value_entries
        * lax.rsqrt(jnp.mean(value_entries * value_entries, axis=1, keepdims=True) + 1e-06)
    ).astype(jnp.bfloat16)
    row_index = jnp.arange(row_count, dtype=jnp.int32)
    earlier = (owners[None, :] == owners[:, None]) & (row_index[None, :] < row_index[:, None])
    arrival = jnp.sum(earlier.astype(jnp.int32), axis=1)
    place = jnp.asarray(np.asarray(pos2dev, np.int32))[owners] * capacity + arrival
    slot_index = jnp.arange(slot_count, dtype=jnp.int32)
    hit = place[None, :] == slot_index[:, None]
    outgoing = jnp.dot(
        hit.astype(jnp.bfloat16), unit, preferred_element_type=jnp.float32
    ).astype(jnp.bfloat16)
    outgoing_ids = jnp.sum(jnp.where(hit, clusters[None, :] + 1, 0), axis=1) - 1
    pair_count = pairs[0].size
    side = jnp.concatenate(
        [
            outgoing_ids.reshape(device_count, capacity),
            jnp.broadcast_to(pairs[0].reshape(1, pair_count), (device_count, pair_count)),
        ],
        axis=1,
    ).astype(jnp.bfloat16)
    id_row = jnp.pad(side, ((0, 0), (0, feature_span - capacity - pair_count)))[:, None, :]
    payload = jnp.concatenate([outgoing.reshape(device_count, capacity, feature_span), id_row], axis=1)
    arrived = lax.all_to_all(payload, "blk", split_axis=0, concat_axis=0, tiled=True)
    own = arrived[:, :capacity].reshape(slot_count, feature_span)
    own_ids = arrived[:, capacity, :capacity].reshape(slot_count).astype(jnp.int32)

    all_pairs = (
        arrived[:, capacity, capacity : capacity + pair_count].astype(jnp.int32).reshape((device_count,) + pairs.shape[1:])
    )
    my_pairs = all_pairs[position]
    ahead_pairs = all_pairs[(position + 2) % device_count]

    n = device_count
    evens = range(0, n, 2)
    half = slot_count // 2
    forward = [(p, (p + 2) % n) for p in range(n)]
    swap = [(p, p ^ 1) for p in range(n)]
    fwd_a = moved(pack(own[:half], own_ids[:half]), pos2dev, forward)
    across = moved(pack(own, own_ids), pos2dev, [(p, p + 1) for p in evens])
    total = step_total(own, own_ids, own, own_ids, my_pairs[0], True)
    total, fwd_a, across = lax.optimization_barrier((total, fwd_a, across))
    _, second_half, packed = lax.optimization_barrier(
        (fwd_a, pack(own[half:], own_ids[half:]), pack(own, own_ids))
    )
    fwd_b = moved(second_half, pos2dev, forward)
    back2 = moved(packed, pos2dev, [(p, (p - 2) % n) for p in evens] + [(p, p) for p in range(1, n, 2)])
    swapped_a = moved(fwd_a, pos2dev, swap)
    across_held, across_ids = unpack(across)

    def half_steps(fwd, swapped, lo, total):
        fwd_held, fwd_ids = unpack(fwd)
        swapped_held, swapped_ids = unpack(swapped)
        q0 = lo // 128
        total = total + step_total(own, own_ids, fwd_held, fwd_ids, my_pairs[2], False, q0)
        return total + step_total(
            own,
            own_ids,
            jnp.where(odd, across_held[lo : lo + half], swapped_held),
            jnp.where(odd, across_ids[lo : lo + half], swapped_ids),
            my_pairs[1],
            False,
            q0,
        )

    def last_step(swapped, lo):
        back2_held, back2_ids = unpack(back2)
        swapped_held, swapped_ids = unpack(swapped)
        return step_total(
            back2_held,
            back2_ids,
            swapped_held,
            swapped_ids,
            jnp.where(odd, my_pairs[3], ahead_pairs[3]),
            False,
            lo // 128,
        )

    total = half_steps(fwd_a, swapped_a, 0, total)
    fwd_b, total = lax.optimization_barrier((fwd_b, total))
    swapped_b = moved(fwd_b, pos2dev, swap)
    total = half_steps(fwd_b, swapped_b, half, total)
    last = last_step(swapped_a, 0) + last_step(swapped_b, half)
    total = total + jnp.where(odd, last, 0.0)
    forward_part = jnp.where(odd, 0.0, last)
    totals = jnp.stack([total.reshape(device_count, capacity), forward_part.reshape(device_count, capacity)], axis=1)
    returned = lax.all_to_all(totals, "blk", split_axis=0, concat_axis=0, tiled=True)
    behind = jnp.asarray(np.asarray(pos2dev, np.int32))[(owners - 2) % device_count] * capacity + arrival
    behind = jnp.where(owners % 2 == 0, behind, -1)
    both = jnp.sum(
        jnp.where(place[:, None] == slot_index[None, :], returned[:, 0].reshape(-1)[None, :], 0.0)
        + jnp.where(behind[:, None] == slot_index[None, :], returned[:, 1].reshape(-1)[None, :], 0.0),
        axis=1,
    )
    return jnp.log1p(both)


def solution(mesh):
    placed = (
        P(("groups", "blk"), None),
        P(("groups", "blk")),
        P(("groups", "blk")),
        P(("groups", "blk"), None, None, None),
    )
    return jax.shard_map(
        body, mesh=mesh, in_specs=placed, out_specs=P(("groups", "blk")), check_vma=False
    )
```

```python
import numpy as np
import jax
import jax.numpy as jnp
from jax import lax
from jax.sharding import PartitionSpec as P

SLOTS = 1024
STEPS = 4
ID_ROWS = 16


SHARPNESS_KNOB = 32.0


def ring_order(n):
    if n == 16:
        chips = [(z, 0) for z in range(4)] + [(z, 1) for z in reversed(range(4))]
        return [chips[p // 2][0] * 4 + chips[p // 2][1] * 2 + p % 2 for p in range(n)]
    return list(range(n))


def moved(x, pos2dev, moves):
    return lax.ppermute(x, "blk", [(pos2dev[a], pos2dev[b]) for a, b in moves])


def step_total(local, local_ids, remote, remote_ids, step_pairs, first_step, first_block=0):
    slot_count, feature_span = local.shape
    block_count = slot_count // 128
    remote_blocks = remote.shape[0] // 128
    logits = lax.dot_general(
        local, remote, (((1,), (1,)), ((), ())), preferred_element_type=jnp.float32
    ) * (SHARPNESS_KNOB / feature_span)
    keep = (local_ids[:, None] == remote_ids[None, :]) & (local_ids[:, None] >= 0)
    if first_step:
        keep = keep & jnp.logical_not(jnp.eye(slot_count, dtype=bool))
    contrib = jnp.where(keep, jnp.exp(logits), 0.0)
    per_block = contrib.reshape(slot_count, remote_blocks, 128).sum(axis=2)
    named = first_block + jnp.arange(remote_blocks, dtype=jnp.int32)
    counts = jnp.sum(step_pairs[:, :, None] == named, axis=1).astype(jnp.float32)
    per_block = per_block.reshape(block_count, 128, remote_blocks)
    return jnp.sum(per_block * counts[:, None, :], axis=2)


def pack(held, held_ids):
    feature_span = held.shape[1]
    id_rows = jnp.pad(held_ids.astype(jnp.bfloat16), (0, ID_ROWS * feature_span - held_ids.shape[0]))
    return jnp.concatenate([held, id_rows.reshape(ID_ROWS, feature_span)], axis=0)


def unpack(packed):
    slot_count = packed.shape[0] - ID_ROWS
    return packed[:slot_count], packed[slot_count:].reshape(-1)[:slot_count].astype(jnp.int32)


def body(embeddings, owners, clusters, pairs):
    device_count = lax.axis_size("blk")
    row_count, feature_span = embeddings.shape
    slot_count = SLOTS
    capacity = slot_count // device_count
    block_count = slot_count // 128
    pos2dev = ring_order(device_count)
    dev2pos = np.argsort(np.asarray(pos2dev)).astype(np.int32)
    position = jnp.asarray(dev2pos)[lax.axis_index("blk")]
    odd = (position % 2) == 1

    value_entries = embeddings.astype(jnp.float32)
    unit = (
        value_entries
        * lax.rsqrt(jnp.mean(value_entries * value_entries, axis=1, keepdims=True) + 1e-06)
    ).astype(jnp.bfloat16)
    row_index = jnp.arange(row_count, dtype=jnp.int32)
    earlier = (owners[None, :] == owners[:, None]) & (row_index[None, :] < row_index[:, None])
    arrival = jnp.sum(earlier.astype(jnp.int32), axis=1)
    place = jnp.asarray(np.asarray(pos2dev, np.int32))[owners] * capacity + arrival
    slot_index = jnp.arange(slot_count, dtype=jnp.int32)
    hit = place[None, :] == slot_index[:, None]
    outgoing = jnp.dot(
        hit.astype(jnp.bfloat16), unit, preferred_element_type=jnp.float32
    ).astype(jnp.bfloat16)
    outgoing_ids = jnp.sum(jnp.where(hit, clusters[None, :] + 1, 0), axis=1) - 1
    pair_count = pairs[0].size
    side = jnp.concatenate(
        [
            outgoing_ids.reshape(device_count, capacity),
            jnp.broadcast_to(pairs[0].reshape(1, pair_count), (device_count, pair_count)),
        ],
        axis=1,
    ).astype(jnp.bfloat16)
    id_row = jnp.pad(side, ((0, 0), (0, feature_span - capacity - pair_count)))[:, None, :]
    payload = jnp.concatenate([outgoing.reshape(device_count, capacity, feature_span), id_row], axis=1)
    arrived = lax.all_to_all(payload, "blk", split_axis=0, concat_axis=0, tiled=True)
    own = arrived[:, :capacity].reshape(slot_count, feature_span)
    own_ids = arrived[:, capacity, :capacity].reshape(slot_count).astype(jnp.int32)

    all_pairs = (
        arrived[:, capacity, capacity : capacity + pair_count].astype(jnp.int32).reshape((device_count,) + pairs.shape[1:])
    )
    my_pairs = all_pairs[position]
    ahead_pairs = all_pairs[(position + 2) % device_count]

    n = device_count
    evens = range(0, n, 2)
    half = slot_count // 2
    forward = [(p, (p + 2) % n) for p in range(n)]
    swap = [(p, p ^ 1) for p in range(n)]
    fwd_a = moved(pack(own[:half], own_ids[:half]), pos2dev, forward)
    across = moved(pack(own, own_ids), pos2dev, [(p, p + 1) for p in evens])
    total = step_total(own, own_ids, own, own_ids, my_pairs[0], True)
    total, across = lax.optimization_barrier((total, across))
    across_held, across_ids = unpack(across)
    from_across = [
        step_total(own, own_ids, across_held[lo : lo + half], across_ids[lo : lo + half], my_pairs[1], False, lo // 128)
        for lo in (0, half)
    ]
    total, fwd_a, from_across = lax.optimization_barrier((total, fwd_a, from_across))
    _, second_half, packed = lax.optimization_barrier(
        (fwd_a, pack(own[half:], own_ids[half:]), pack(own, own_ids))
    )
    fwd_b = moved(second_half, pos2dev, forward)
    back2 = moved(packed, pos2dev, [(p, (p - 2) % n) for p in evens] + [(p, p) for p in range(1, n, 2)])
    swapped_a = moved(fwd_a, pos2dev, swap)

    def half_steps(fwd, swapped, lo, total):
        fwd_held, fwd_ids = unpack(fwd)
        swapped_held, swapped_ids = unpack(swapped)
        q0 = lo // 128
        total = total + step_total(own, own_ids, fwd_held, fwd_ids, my_pairs[2], False, q0)
        from_swap = step_total(own, own_ids, swapped_held, swapped_ids, my_pairs[1], False, q0)
        return total + jnp.where(odd, from_across[lo // half], from_swap)

    def last_step(swapped, lo):
        back2_held, back2_ids = unpack(back2)
        swapped_held, swapped_ids = unpack(swapped)
        return step_total(
            back2_held,
            back2_ids,
            swapped_held,
            swapped_ids,
            jnp.where(odd, my_pairs[3], ahead_pairs[3]),
            False,
            lo // 128,
        )

    total = half_steps(fwd_a, swapped_a, 0, total)
    fwd_b, total = lax.optimization_barrier((fwd_b, total))
    swapped_b = moved(fwd_b, pos2dev, swap)
    total = half_steps(fwd_b, swapped_b, half, total)
    last = last_step(swapped_a, 0) + last_step(swapped_b, half)
    total = total + jnp.where(odd, last, 0.0)
    forward_part = jnp.where(odd, 0.0, last)
    totals = jnp.stack([total.reshape(device_count, capacity), forward_part.reshape(device_count, capacity)], axis=1)
    returned = lax.all_to_all(totals, "blk", split_axis=0, concat_axis=0, tiled=True)
    behind = jnp.asarray(np.asarray(pos2dev, np.int32))[(owners - 2) % device_count] * capacity + arrival
    behind = jnp.where(owners % 2 == 0, behind, -1)
    both = jnp.sum(
        jnp.where(place[:, None] == slot_index[None, :], returned[:, 0].reshape(-1)[None, :], 0.0)
        + jnp.where(behind[:, None] == slot_index[None, :], returned[:, 1].reshape(-1)[None, :], 0.0),
        axis=1,
    )
    return jnp.log1p(both)


def solution(mesh):
    placed = (
        P(("groups", "blk"), None),
        P(("groups", "blk")),
        P(("groups", "blk")),
        P(("groups", "blk"), None, None, None),
    )
    return jax.shard_map(
        body, mesh=mesh, in_specs=placed, out_specs=P(("groups", "blk")), check_vma=False
    )
```

```python
import numpy as np
import jax
import jax.numpy as jnp
from jax import lax
from jax.sharding import PartitionSpec as P

SLOTS = 1024
STEPS = 4
ID_ROWS = 16


SHARPNESS_KNOB = 32.0


def ring_order(n):
    if n == 16:
        chips = [(z, 0) for z in range(4)] + [(z, 1) for z in reversed(range(4))]
        return [chips[p // 2][0] * 4 + chips[p // 2][1] * 2 + p % 2 for p in range(n)]
    return list(range(n))


def moved(x, pos2dev, moves):
    return lax.ppermute(x, "blk", [(pos2dev[a], pos2dev[b]) for a, b in moves])


def step_total(local, local_ids, remote, remote_ids, step_pairs, first_step, first_block=0):
    slot_count, feature_span = local.shape
    block_count = slot_count // 128
    remote_blocks = remote.shape[0] // 128
    logits = lax.dot_general(
        local, remote, (((1,), (1,)), ((), ())), preferred_element_type=jnp.float32
    ) * (SHARPNESS_KNOB / feature_span)
    keep = (local_ids[:, None] == remote_ids[None, :]) & (local_ids[:, None] >= 0)
    if first_step:
        keep = keep & jnp.logical_not(jnp.eye(slot_count, dtype=bool))
    contrib = jnp.where(keep, jnp.exp(logits), 0.0)
    per_block = contrib.reshape(slot_count, remote_blocks, 128).sum(axis=2)
    named = first_block + jnp.arange(remote_blocks, dtype=jnp.int32)
    counts = jnp.sum(step_pairs[:, :, None] == named, axis=1).astype(jnp.float32)
    per_block = per_block.reshape(block_count, 128, remote_blocks)
    return jnp.sum(per_block * counts[:, None, :], axis=2)


def pack(held, held_ids):
    feature_span = held.shape[1]
    id_rows = jnp.pad(held_ids.astype(jnp.bfloat16), (0, ID_ROWS * feature_span - held_ids.shape[0]))
    return jnp.concatenate([held, id_rows.reshape(ID_ROWS, feature_span)], axis=0)


def unpack(packed):
    slot_count = packed.shape[0] - ID_ROWS
    return packed[:slot_count], packed[slot_count:].reshape(-1)[:slot_count].astype(jnp.int32)


def body(embeddings, owners, clusters, pairs):
    device_count = lax.axis_size("blk")
    row_count, feature_span = embeddings.shape
    slot_count = SLOTS
    capacity = slot_count // device_count
    block_count = slot_count // 128
    pos2dev = ring_order(device_count)
    dev2pos = np.argsort(np.asarray(pos2dev)).astype(np.int32)
    position = jnp.asarray(dev2pos)[lax.axis_index("blk")]
    odd = (position % 2) == 1

    value_entries = embeddings.astype(jnp.float32)
    unit = (
        value_entries
        * lax.rsqrt(jnp.mean(value_entries * value_entries, axis=1, keepdims=True) + 1e-06)
    ).astype(jnp.bfloat16)
    row_index = jnp.arange(row_count, dtype=jnp.int32)
    earlier = (owners[None, :] == owners[:, None]) & (row_index[None, :] < row_index[:, None])
    arrival = jnp.sum(earlier.astype(jnp.int32), axis=1)
    place = jnp.asarray(np.asarray(pos2dev, np.int32))[owners] * capacity + arrival
    slot_index = jnp.arange(slot_count, dtype=jnp.int32)
    hit = place[None, :] == slot_index[:, None]
    outgoing = jnp.dot(
        hit.astype(jnp.bfloat16), unit, preferred_element_type=jnp.float32
    ).astype(jnp.bfloat16)
    outgoing_ids = jnp.sum(jnp.where(hit, clusters[None, :] + 1, 0), axis=1) - 1
    pair_count = pairs[0].size
    side = jnp.concatenate(
        [
            outgoing_ids.reshape(device_count, capacity),
            jnp.broadcast_to(pairs[0].reshape(1, pair_count), (device_count, pair_count)),
        ],
        axis=1,
    ).astype(jnp.bfloat16)
    id_row = jnp.pad(side, ((0, 0), (0, feature_span - capacity - pair_count)))[:, None, :]
    payload = jnp.concatenate([outgoing.reshape(device_count, capacity, feature_span), id_row], axis=1)
    arrived = lax.all_to_all(payload, "blk", split_axis=0, concat_axis=0, tiled=True)
    own = arrived[:, :capacity].reshape(slot_count, feature_span)
    own_ids = arrived[:, capacity, :capacity].reshape(slot_count).astype(jnp.int32)

    all_pairs = (
        arrived[:, capacity, capacity : capacity + pair_count].astype(jnp.int32).reshape((device_count,) + pairs.shape[1:])
    )
    my_pairs = all_pairs[position]
    ahead_pairs = all_pairs[(position + 2) % device_count]

    n = device_count
    evens = range(0, n, 2)
    half = slot_count // 2
    forward = [(p, (p + 2) % n) for p in range(n)]
    swap = [(p, p ^ 1) for p in range(n)]
    fwd_a = moved(pack(own[:half], own_ids[:half]), pos2dev, forward)
    across = moved(pack(own, own_ids), pos2dev, [(p, p + 1) for p in evens])
    total = step_total(own, own_ids, own, own_ids, my_pairs[0], True)
    total, across = lax.optimization_barrier((total, across))
    across_held, across_ids = unpack(across)
    from_across = [
        step_total(own, own_ids, across_held[lo : lo + half], across_ids[lo : lo + half], my_pairs[1], False, lo // 128)
        for lo in (0, half)
    ]
    total, fwd_a, from_across = lax.optimization_barrier((total, fwd_a, from_across))
    _, second_half, packed = lax.optimization_barrier(
        (fwd_a, pack(own[half:], own_ids[half:]), pack(own, own_ids))
    )
    fwd_b = moved(second_half, pos2dev, forward)
    back2 = moved(packed, pos2dev, [(p, (p - 2) % n) for p in evens] + [(p, p) for p in range(1, n, 2)])
    swapped_a = moved(fwd_a, pos2dev, swap)

    def half_steps(fwd, swapped, lo, total):
        fwd_held, fwd_ids = unpack(fwd)
        swapped_held, swapped_ids = unpack(swapped)
        q0 = lo // 128
        total = total + step_total(own, own_ids, fwd_held, fwd_ids, my_pairs[2], False, q0)
        from_swap = step_total(own, own_ids, swapped_held, swapped_ids, my_pairs[1], False, q0)
        return total + jnp.where(odd, from_across[lo // half], from_swap)

    def last_step(swapped, lo):
        back2_held, back2_ids = unpack(back2)
        swapped_held, swapped_ids = unpack(swapped)
        return step_total(
            back2_held,
            back2_ids,
            swapped_held,
            swapped_ids,
            jnp.where(odd, my_pairs[3], ahead_pairs[3]),
            False,
            lo // 128,
        )

    total = half_steps(fwd_a, swapped_a, 0, total)
    fwd_b, total = lax.optimization_barrier((fwd_b, total))
    swapped_b = moved(fwd_b, pos2dev, swap)
    total = half_steps(fwd_b, swapped_b, half, total)
    last = last_step(swapped_a, 0) + last_step(swapped_b, half)
    total = total + jnp.where(odd, last, 0.0)
    forward_part = jnp.where(odd, 0.0, last)
    totals = jnp.stack([total.reshape(device_count, capacity), forward_part.reshape(device_count, capacity)], axis=1)
    returned = lax.all_to_all(totals, "blk", split_axis=0, concat_axis=0, tiled=True)
    ring_dev = jnp.asarray(np.asarray(pos2dev, np.int32))
    source_dev = jnp.stack([ring_dev[owners], jnp.where(owners % 2 == 0, ring_dev[(owners - 2) % device_count], -1)], axis=1)
    dev_index = jnp.arange(device_count, dtype=jnp.int32)
    slot_in = jnp.arange(capacity, dtype=jnp.int32)
    pick = (
        (source_dev[:, None, :, None] == dev_index[None, :, None, None])
        & (arrival[:, None, None, None] == slot_in[None, None, None, :])
    ).astype(jnp.float32)
    both = jnp.einsum("rePa,ePa->r", pick, returned, precision=lax.Precision.HIGHEST)
    return jnp.log1p(both)


def solution(mesh):
    placed = (
        P(("groups", "blk"), None),
        P(("groups", "blk")),
        P(("groups", "blk")),
        P(("groups", "blk"), None, None, None),
    )
    return jax.shard_map(
        body, mesh=mesh, in_specs=placed, out_specs=P(("groups", "blk")), check_vma=False
    )
```

```python
import numpy as np
import jax
import jax.numpy as jnp
from jax import lax
from jax.sharding import PartitionSpec as P

SLOTS = 1024
STEPS = 4
ID_ROWS = 16


SHARPNESS_KNOB = 32.0


def ring_order(n):
    if n == 16:
        chips = [(z, 0) for z in range(4)] + [(z, 1) for z in reversed(range(4))]
        return [chips[p // 2][0] * 4 + chips[p // 2][1] * 2 + p % 2 for p in range(n)]
    return list(range(n))


def moved(x, pos2dev, moves):
    return lax.ppermute(x, "blk", [(pos2dev[a], pos2dev[b]) for a, b in moves])


def step_total(local, local_ids, remote, remote_ids, step_pairs, first_step, first_block=0):
    slot_count, feature_span = local.shape
    block_count = slot_count // 128
    remote_blocks = remote.shape[0] // 128
    logits = lax.dot_general(
        local, remote, (((1,), (1,)), ((), ())), preferred_element_type=jnp.float32
    ) * (SHARPNESS_KNOB / feature_span)
    keep = (local_ids[:, None] == remote_ids[None, :]) & (local_ids[:, None] >= 0)
    if first_step:
        keep = keep & jnp.logical_not(jnp.eye(slot_count, dtype=bool))
    contrib = jnp.where(keep, jnp.exp(logits), 0.0)
    per_block = contrib.reshape(slot_count, remote_blocks, 128).sum(axis=2)
    named = first_block + jnp.arange(remote_blocks, dtype=jnp.int32)
    counts = jnp.sum(step_pairs[:, :, None] == named, axis=1).astype(jnp.float32)
    per_block = per_block.reshape(block_count, 128, remote_blocks)
    return jnp.sum(per_block * counts[:, None, :], axis=2)


def pack(held, held_ids):
    feature_span = held.shape[1]
    id_rows = jnp.pad(held_ids.astype(jnp.bfloat16), (0, ID_ROWS * feature_span - held_ids.shape[0]))
    return jnp.concatenate([held, id_rows.reshape(ID_ROWS, feature_span)], axis=0)


def unpack(packed):
    slot_count = packed.shape[0] - ID_ROWS
    return packed[:slot_count], packed[slot_count:].reshape(-1)[:slot_count].astype(jnp.int32)


def body(embeddings, owners, clusters, pairs):
    device_count = lax.axis_size("blk")
    row_count, feature_span = embeddings.shape
    slot_count = SLOTS
    capacity = slot_count // device_count
    block_count = slot_count // 128
    pos2dev = ring_order(device_count)
    dev2pos = np.argsort(np.asarray(pos2dev)).astype(np.int32)
    position = jnp.asarray(dev2pos)[lax.axis_index("blk")]
    odd = (position % 2) == 1

    value_entries = embeddings.astype(jnp.float32)
    unit = (
        value_entries
        * lax.rsqrt(jnp.mean(value_entries * value_entries, axis=1, keepdims=True) + 1e-06)
    ).astype(jnp.bfloat16)
    row_index = jnp.arange(row_count, dtype=jnp.int32)
    earlier = (owners[None, :] == owners[:, None]) & (row_index[None, :] < row_index[:, None])
    arrival = jnp.sum(earlier.astype(jnp.int32), axis=1)
    place = jnp.asarray(np.asarray(pos2dev, np.int32))[owners] * capacity + arrival
    slot_index = jnp.arange(slot_count, dtype=jnp.int32)
    hit = place[None, :] == slot_index[:, None]
    outgoing = jnp.dot(
        hit.astype(jnp.bfloat16), unit, preferred_element_type=jnp.float32
    ).astype(jnp.bfloat16)
    outgoing_ids = jnp.sum(jnp.where(hit, clusters[None, :] + 1, 0), axis=1) - 1
    pair_count = pairs[0].size
    side = jnp.concatenate(
        [
            outgoing_ids.reshape(device_count, capacity),
            jnp.broadcast_to(pairs[0].reshape(1, pair_count), (device_count, pair_count)),
        ],
        axis=1,
    ).astype(jnp.bfloat16)
    id_row = jnp.pad(side, ((0, 0), (0, feature_span - capacity - pair_count)))[:, None, :]
    payload = jnp.concatenate([outgoing.reshape(device_count, capacity, feature_span), id_row], axis=1)
    arrived = lax.all_to_all(payload, "blk", split_axis=0, concat_axis=0, tiled=True)
    own = arrived[:, :capacity].reshape(slot_count, feature_span)
    own_ids = arrived[:, capacity, :capacity].reshape(slot_count).astype(jnp.int32)

    all_pairs = (
        arrived[:, capacity, capacity : capacity + pair_count].astype(jnp.int32).reshape((device_count,) + pairs.shape[1:])
    )
    my_pairs = all_pairs[position]
    ahead_pairs = all_pairs[(position + 2) % device_count]

    n = device_count
    evens = range(0, n, 2)
    half = slot_count // 2
    forward = [(p, (p + 2) % n) for p in range(n)]
    swap = [(p, p ^ 1) for p in range(n)]
    fwd_a = moved(pack(own[:half], own_ids[:half]), pos2dev, forward)
    across = moved(pack(own, own_ids), pos2dev, [(p, p + 1) for p in evens])
    back2 = moved(pack(own, own_ids), pos2dev, [(p, (p - 2) % n) for p in evens] + [(p, p) for p in range(1, n, 2)])
    total = step_total(own, own_ids, own, own_ids, my_pairs[0], True)
    total, across, back2 = lax.optimization_barrier((total, across, back2))
    across_held, across_ids = unpack(across)
    from_across = [
        step_total(own, own_ids, across_held[lo : lo + half], across_ids[lo : lo + half], my_pairs[1], False, lo // 128)
        for lo in (0, half)
    ]
    total, fwd_a, from_across = lax.optimization_barrier((total, fwd_a, from_across))
    _, second_half, packed = lax.optimization_barrier(
        (fwd_a, pack(own[half:], own_ids[half:]), pack(own, own_ids))
    )
    fwd_b = moved(second_half, pos2dev, forward)
    swapped_a = moved(fwd_a, pos2dev, swap)

    def half_steps(fwd, swapped, lo, total):
        fwd_held, fwd_ids = unpack(fwd)
        swapped_held, swapped_ids = unpack(swapped)
        q0 = lo // 128
        total = total + step_total(own, own_ids, fwd_held, fwd_ids, my_pairs[2], False, q0)
        from_swap = step_total(own, own_ids, swapped_held, swapped_ids, my_pairs[1], False, q0)
        return total + jnp.where(odd, from_across[lo // half], from_swap)

    def last_step(swapped, lo):
        back2_held, back2_ids = unpack(back2)
        swapped_held, swapped_ids = unpack(swapped)
        return step_total(
            back2_held,
            back2_ids,
            swapped_held,
            swapped_ids,
            jnp.where(odd, my_pairs[3], ahead_pairs[3]),
            False,
            lo // 128,
        )

    total = half_steps(fwd_a, swapped_a, 0, total)
    last = last_step(swapped_a, 0)
    fwd_b, total, last = lax.optimization_barrier((fwd_b, total, last))
    swapped_b = moved(fwd_b, pos2dev, swap)
    total = half_steps(fwd_b, swapped_b, half, total)
    last = last + last_step(swapped_b, half)
    total = total + jnp.where(odd, last, 0.0)
    forward_part = jnp.where(odd, 0.0, last)
    totals = jnp.stack([total.reshape(device_count, capacity), forward_part.reshape(device_count, capacity)], axis=1)
    returned = lax.all_to_all(totals, "blk", split_axis=0, concat_axis=0, tiled=True)
    behind = jnp.asarray(np.asarray(pos2dev, np.int32))[(owners - 2) % device_count] * capacity + arrival
    behind = jnp.where(owners % 2 == 0, behind, -1)
    both = jnp.sum(
        jnp.where(place[:, None] == slot_index[None, :], returned[:, 0].reshape(-1)[None, :], 0.0)
        + jnp.where(behind[:, None] == slot_index[None, :], returned[:, 1].reshape(-1)[None, :], 0.0),
        axis=1,
    )
    return jnp.log1p(both)


def solution(mesh):
    placed = (
        P(("groups", "blk"), None),
        P(("groups", "blk")),
        P(("groups", "blk")),
        P(("groups", "blk"), None, None, None),
    )
    return jax.shard_map(
        body, mesh=mesh, in_specs=placed, out_specs=P(("groups", "blk")), check_vma=False
    )
```

```python
import numpy as np
import jax
import jax.numpy as jnp
from jax import lax
from jax.sharding import PartitionSpec as P

SLOTS = 1024
STEPS = 4
ID_ROWS = 16


SHARPNESS_KNOB = 32.0


def ring_order(n):
    if n == 16:
        chips = [(z, 0) for z in range(4)] + [(z, 1) for z in reversed(range(4))]
        return [chips[p // 2][0] * 4 + chips[p // 2][1] * 2 + p % 2 for p in range(n)]
    return list(range(n))


def moved(x, pos2dev, moves):
    return lax.ppermute(x, "blk", [(pos2dev[a], pos2dev[b]) for a, b in moves])


def step_total(local, local_ids, remote, remote_ids, step_pairs, first_step, first_block=0):
    slot_count, feature_span = local.shape
    block_count = slot_count // 128
    remote_blocks = remote.shape[0] // 128
    logits = lax.dot_general(
        local, remote, (((1,), (1,)), ((), ())), preferred_element_type=jnp.float32
    ) * (SHARPNESS_KNOB / feature_span)
    keep = (local_ids[:, None] == remote_ids[None, :]) & (local_ids[:, None] >= 0)
    if first_step:
        keep = keep & jnp.logical_not(jnp.eye(slot_count, dtype=bool))
    contrib = jnp.where(keep, jnp.exp(logits), 0.0)
    per_block = contrib.reshape(slot_count, remote_blocks, 128).sum(axis=2)
    named = first_block + jnp.arange(remote_blocks, dtype=jnp.int32)
    counts = jnp.sum(step_pairs[:, :, None] == named, axis=1).astype(jnp.float32)
    per_block = per_block.reshape(block_count, 128, remote_blocks)
    return jnp.sum(per_block * counts[:, None, :], axis=2)


def pack(held, held_ids):
    feature_span = held.shape[1]
    id_rows = jnp.pad(held_ids.astype(jnp.bfloat16), (0, ID_ROWS * feature_span - held_ids.shape[0]))
    return jnp.concatenate([held, id_rows.reshape(ID_ROWS, feature_span)], axis=0)


def unpack(packed):
    slot_count = packed.shape[0] - ID_ROWS
    return packed[:slot_count], packed[slot_count:].reshape(-1)[:slot_count].astype(jnp.int32)


def body(embeddings, owners, clusters, pairs):
    device_count = lax.axis_size("blk")
    row_count, feature_span = embeddings.shape
    slot_count = SLOTS
    capacity = slot_count // device_count
    block_count = slot_count // 128
    pos2dev = ring_order(device_count)
    dev2pos = np.argsort(np.asarray(pos2dev)).astype(np.int32)
    position = jnp.asarray(dev2pos)[lax.axis_index("blk")]
    odd = (position % 2) == 1

    value_entries = embeddings.astype(jnp.float32)
    unit = (
        value_entries
        * lax.rsqrt(jnp.mean(value_entries * value_entries, axis=1, keepdims=True) + 1e-06)
    ).astype(jnp.bfloat16)
    row_index = jnp.arange(row_count, dtype=jnp.int32)
    earlier = (owners[None, :] == owners[:, None]) & (row_index[None, :] < row_index[:, None])
    arrival = jnp.sum(earlier.astype(jnp.int32), axis=1)
    place = jnp.asarray(np.asarray(pos2dev, np.int32))[owners] * capacity + arrival
    slot_index = jnp.arange(slot_count, dtype=jnp.int32)
    hit = place[None, :] == slot_index[:, None]
    outgoing = jnp.dot(
        hit.astype(jnp.bfloat16), unit, preferred_element_type=jnp.float32
    ).astype(jnp.bfloat16)
    outgoing_ids = jnp.sum(jnp.where(hit, clusters[None, :] + 1, 0), axis=1) - 1
    pair_count = pairs[0].size
    side = jnp.concatenate(
        [
            outgoing_ids.reshape(device_count, capacity),
            jnp.broadcast_to(pairs[0].reshape(1, pair_count), (device_count, pair_count)),
        ],
        axis=1,
    ).astype(jnp.bfloat16)
    id_row = jnp.pad(side, ((0, 0), (0, feature_span - capacity - pair_count)))[:, None, :]
    payload = jnp.concatenate([outgoing.reshape(device_count, capacity, feature_span), id_row], axis=1)
    arrived = lax.all_to_all(payload, "blk", split_axis=0, concat_axis=0, tiled=True)
    own = arrived[:, :capacity].reshape(slot_count, feature_span)
    own_ids = arrived[:, capacity, :capacity].reshape(slot_count).astype(jnp.int32)

    all_pairs = (
        arrived[:, capacity, capacity : capacity + pair_count].astype(jnp.int32).reshape((device_count,) + pairs.shape[1:])
    )
    my_pairs = all_pairs[position]
    ahead_pairs = all_pairs[(position + 2) % device_count]

    n = device_count
    evens = range(0, n, 2)
    half = slot_count // 2
    forward = [(p, (p + 2) % n) for p in range(n)]
    swap = [(p, p ^ 1) for p in range(n)]
    fwd_a = moved(pack(own[:half], own_ids), pos2dev, forward)
    across = moved(pack(own, own_ids), pos2dev, [(p, p + 1) for p in evens])
    total = step_total(own, own_ids, own, own_ids, my_pairs[0], True)
    total, across = lax.optimization_barrier((total, across))
    across_held, across_ids = unpack(across)
    from_across = [
        step_total(own, own_ids, across_held[lo : lo + half], across_ids[lo : lo + half], my_pairs[1], False, lo // 128)
        for lo in (0, half)
    ]
    total, fwd_a, from_across = lax.optimization_barrier((total, fwd_a, from_across))
    _, second_half, packed = lax.optimization_barrier((fwd_a, own[half:], pack(own, own_ids)))
    fwd_b = moved(second_half, pos2dev, forward)
    back2 = moved(packed, pos2dev, [(p, (p - 2) % n) for p in evens] + [(p, p) for p in range(1, n, 2)])
    swapped_a = moved(fwd_a, pos2dev, swap)

    def all_ids(packed_half):
        return packed_half[half:].reshape(-1)[:slot_count].astype(jnp.int32)

    fwd_all_ids = all_ids(fwd_a)
    swapped_all_ids = all_ids(swapped_a)

    def half_steps(fwd, swapped, lo, total):
        fwd_held, fwd_ids = fwd[:half], fwd_all_ids[lo : lo + half]
        swapped_held, swapped_ids = swapped[:half], swapped_all_ids[lo : lo + half]
        q0 = lo // 128
        total = total + step_total(own, own_ids, fwd_held, fwd_ids, my_pairs[2], False, q0)
        from_swap = step_total(own, own_ids, swapped_held, swapped_ids, my_pairs[1], False, q0)
        return total + jnp.where(odd, from_across[lo // half], from_swap)

    def last_step(swapped, lo):
        back2_held, back2_ids = unpack(back2)
        swapped_held, swapped_ids = swapped[:half], swapped_all_ids[lo : lo + half]
        return step_total(
            back2_held,
            back2_ids,
            swapped_held,
            swapped_ids,
            jnp.where(odd, my_pairs[3], ahead_pairs[3]),
            False,
            lo // 128,
        )

    total = half_steps(fwd_a, swapped_a, 0, total)
    fwd_b, total = lax.optimization_barrier((fwd_b, total))
    swapped_b = moved(fwd_b, pos2dev, swap)
    total = half_steps(fwd_b, swapped_b, half, total)
    last = last_step(swapped_a, 0) + last_step(swapped_b, half)
    total = total + jnp.where(odd, last, 0.0)
    forward_part = jnp.where(odd, 0.0, last)
    totals = jnp.stack([total.reshape(device_count, capacity), forward_part.reshape(device_count, capacity)], axis=1)
    returned = lax.all_to_all(totals, "blk", split_axis=0, concat_axis=0, tiled=True)
    behind = jnp.asarray(np.asarray(pos2dev, np.int32))[(owners - 2) % device_count] * capacity + arrival
    behind = jnp.where(owners % 2 == 0, behind, -1)
    both = jnp.sum(
        jnp.where(place[:, None] == slot_index[None, :], returned[:, 0].reshape(-1)[None, :], 0.0)
        + jnp.where(behind[:, None] == slot_index[None, :], returned[:, 1].reshape(-1)[None, :], 0.0),
        axis=1,
    )
    return jnp.log1p(both)


def solution(mesh):
    placed = (
        P(("groups", "blk"), None),
        P(("groups", "blk")),
        P(("groups", "blk")),
        P(("groups", "blk"), None, None, None),
    )
    return jax.shard_map(
        body, mesh=mesh, in_specs=placed, out_specs=P(("groups", "blk")), check_vma=False
    )
```

```python
import numpy as np
import jax
import jax.numpy as jnp
from jax import lax
from jax.sharding import PartitionSpec as P

SLOTS = 1024
STEPS = 4
ID_ROWS = 16


SHARPNESS_KNOB = 32.0


def ring_order(n):
    if n == 16:
        chips = [(z, 0) for z in range(4)] + [(z, 1) for z in reversed(range(4))]
        return [chips[p // 2][0] * 4 + chips[p // 2][1] * 2 + p % 2 for p in range(n)]
    return list(range(n))


def moved(x, pos2dev, moves):
    return lax.ppermute(x, "blk", [(pos2dev[a], pos2dev[b]) for a, b in moves])


def step_total(local, local_ids, remote, remote_ids, step_pairs, first_step, first_block=0):
    slot_count, feature_span = local.shape
    block_count = slot_count // 128
    remote_blocks = remote.shape[0] // 128
    logits = lax.dot_general(
        local, remote, (((1,), (1,)), ((), ())), preferred_element_type=jnp.float32
    ) * (SHARPNESS_KNOB / feature_span)
    keep = (local_ids[:, None] == remote_ids[None, :]) & (local_ids[:, None] >= 0)
    if first_step:
        keep = keep & jnp.logical_not(jnp.eye(slot_count, dtype=bool))
    contrib = jnp.where(keep, jnp.exp(logits), 0.0)
    per_block = contrib.reshape(slot_count, remote_blocks, 128).sum(axis=2)
    named = first_block + jnp.arange(remote_blocks, dtype=jnp.int32)
    counts = jnp.sum(step_pairs[:, :, None] == named, axis=1).astype(jnp.float32)
    per_block = per_block.reshape(block_count, 128, remote_blocks)
    return jnp.sum(per_block * counts[:, None, :], axis=2)


def pack(held, held_ids):
    feature_span = held.shape[1]
    id_rows = jnp.pad(held_ids.astype(jnp.bfloat16), (0, ID_ROWS * feature_span - held_ids.shape[0]))
    return jnp.concatenate([held, id_rows.reshape(ID_ROWS, feature_span)], axis=0)


def unpack(packed):
    slot_count = packed.shape[0] - ID_ROWS
    return packed[:slot_count], packed[slot_count:].reshape(-1)[:slot_count].astype(jnp.int32)


def body(embeddings, owners, clusters, pairs):
    device_count = lax.axis_size("blk")
    row_count, feature_span = embeddings.shape
    slot_count = SLOTS
    capacity = slot_count // device_count
    block_count = slot_count // 128
    pos2dev = ring_order(device_count)
    dev2pos = np.argsort(np.asarray(pos2dev)).astype(np.int32)
    position = jnp.asarray(dev2pos)[lax.axis_index("blk")]
    odd = (position % 2) == 1

    value_entries = embeddings.astype(jnp.float32)
    unit = (
        value_entries
        * lax.rsqrt(jnp.mean(value_entries * value_entries, axis=1, keepdims=True) + 1e-06)
    ).astype(jnp.bfloat16)
    row_index = jnp.arange(row_count, dtype=jnp.int32)
    earlier = (owners[None, :] == owners[:, None]) & (row_index[None, :] < row_index[:, None])
    arrival = jnp.sum(earlier.astype(jnp.int32), axis=1)
    place = jnp.asarray(np.asarray(pos2dev, np.int32))[owners] * capacity + arrival
    slot_index = jnp.arange(slot_count, dtype=jnp.int32)
    hit = place[None, :] == slot_index[:, None]
    source_row = jnp.sum(jnp.where(hit, row_index[None, :] + 1, 0), axis=1) - 1
    outgoing = jnp.take(unit, jnp.where(source_row < 0, row_count, source_row), axis=0, mode="fill", fill_value=0)
    outgoing_ids = jnp.sum(jnp.where(hit, clusters[None, :] + 1, 0), axis=1) - 1
    pair_count = pairs[0].size
    side = jnp.concatenate(
        [
            outgoing_ids.reshape(device_count, capacity),
            jnp.broadcast_to(pairs[0].reshape(1, pair_count), (device_count, pair_count)),
        ],
        axis=1,
    ).astype(jnp.bfloat16)
    id_row = jnp.pad(side, ((0, 0), (0, feature_span - capacity - pair_count)))[:, None, :]
    payload = jnp.concatenate([outgoing.reshape(device_count, capacity, feature_span), id_row], axis=1)
    arrived = lax.all_to_all(payload, "blk", split_axis=0, concat_axis=0, tiled=True)
    own = arrived[:, :capacity].reshape(slot_count, feature_span)
    own_ids = arrived[:, capacity, :capacity].reshape(slot_count).astype(jnp.int32)

    all_pairs = (
        arrived[:, capacity, capacity : capacity + pair_count].astype(jnp.int32).reshape((device_count,) + pairs.shape[1:])
    )
    my_pairs = all_pairs[position]
    ahead_pairs = all_pairs[(position + 2) % device_count]

    n = device_count
    evens = range(0, n, 2)
    half = slot_count // 2
    forward = [(p, (p + 2) % n) for p in range(n)]
    swap = [(p, p ^ 1) for p in range(n)]
    fwd_a = moved(pack(own[:half], own_ids), pos2dev, forward)
    across = moved(pack(own, own_ids), pos2dev, [(p, p + 1) for p in evens])
    total = step_total(own, own_ids, own, own_ids, my_pairs[0], True)
    total, across = lax.optimization_barrier((total, across))
    across_held, across_ids = unpack(across)
    from_across = [
        step_total(own, own_ids, across_held[lo : lo + half], across_ids[lo : lo + half], my_pairs[1], False, lo // 128)
        for lo in (0, half)
    ]
    total, fwd_a, from_across = lax.optimization_barrier((total, fwd_a, from_across))
    _, second_half, packed = lax.optimization_barrier((fwd_a, own[half:], pack(own, own_ids)))
    fwd_b = moved(second_half, pos2dev, forward)
    back2 = moved(packed, pos2dev, [(p, (p - 2) % n) for p in evens] + [(p, p) for p in range(1, n, 2)])
    swapped_a = moved(fwd_a, pos2dev, swap)

    def all_ids(packed_half):
        return packed_half[half:].reshape(-1)[:slot_count].astype(jnp.int32)

    fwd_all_ids = all_ids(fwd_a)
    swapped_all_ids = all_ids(swapped_a)

    def half_steps(fwd, swapped, lo, total):
        fwd_held, fwd_ids = fwd[:half], fwd_all_ids[lo : lo + half]
        swapped_held, swapped_ids = swapped[:half], swapped_all_ids[lo : lo + half]
        q0 = lo // 128
        total = total + step_total(own, own_ids, fwd_held, fwd_ids, my_pairs[2], False, q0)
        from_swap = step_total(own, own_ids, swapped_held, swapped_ids, my_pairs[1], False, q0)
        return total + jnp.where(odd, from_across[lo // half], from_swap)

    def last_step(swapped, lo):
        back2_held, back2_ids = unpack(back2)
        swapped_held, swapped_ids = swapped[:half], swapped_all_ids[lo : lo + half]
        return step_total(
            back2_held,
            back2_ids,
            swapped_held,
            swapped_ids,
            jnp.where(odd, my_pairs[3], ahead_pairs[3]),
            False,
            lo // 128,
        )

    total = half_steps(fwd_a, swapped_a, 0, total)
    fwd_b, total = lax.optimization_barrier((fwd_b, total))
    swapped_b = moved(fwd_b, pos2dev, swap)
    total = half_steps(fwd_b, swapped_b, half, total)
    last = last_step(swapped_a, 0) + last_step(swapped_b, half)
    total = total + jnp.where(odd, last, 0.0)
    forward_part = jnp.where(odd, 0.0, last)
    totals = jnp.stack([total.reshape(device_count, capacity), forward_part.reshape(device_count, capacity)], axis=1)
    returned = lax.all_to_all(totals, "blk", split_axis=0, concat_axis=0, tiled=True)
    behind = jnp.asarray(np.asarray(pos2dev, np.int32))[(owners - 2) % device_count] * capacity + arrival
    behind = jnp.where(owners % 2 == 0, behind, -1)
    both = jnp.sum(
        jnp.where(place[:, None] == slot_index[None, :], returned[:, 0].reshape(-1)[None, :], 0.0)
        + jnp.where(behind[:, None] == slot_index[None, :], returned[:, 1].reshape(-1)[None, :], 0.0),
        axis=1,
    )
    return jnp.log1p(both)


def solution(mesh):
    placed = (
        P(("groups", "blk"), None),
        P(("groups", "blk")),
        P(("groups", "blk")),
        P(("groups", "blk"), None, None, None),
    )
    return jax.shard_map(
        body, mesh=mesh, in_specs=placed, out_specs=P(("groups", "blk")), check_vma=False
    )
```

```python
import numpy as np
import jax
import jax.numpy as jnp
from jax import lax
from jax.sharding import PartitionSpec as P

SLOTS = 1024
STEPS = 4
ID_ROWS = 16


SHARPNESS_KNOB = 32.0


def ring_order(n):
    if n == 16:
        chips = [(z, 0) for z in range(4)] + [(z, 1) for z in reversed(range(4))]
        return [chips[p // 2][0] * 4 + chips[p // 2][1] * 2 + p % 2 for p in range(n)]
    return list(range(n))


def moved(x, pos2dev, moves):
    return lax.ppermute(x, "blk", [(pos2dev[a], pos2dev[b]) for a, b in moves])


def step_total(local, local_ids, remote, remote_ids, step_pairs, first_step, first_block=0):
    slot_count, feature_span = local.shape
    block_count = slot_count // 128
    remote_blocks = remote.shape[0] // 128
    logits = lax.dot_general(
        local, remote, (((1,), (1,)), ((), ())), preferred_element_type=jnp.float32
    ) * (SHARPNESS_KNOB / feature_span)
    keep = (local_ids[:, None] == remote_ids[None, :]) & (local_ids[:, None] >= 0)
    if first_step:
        keep = keep & jnp.logical_not(jnp.eye(slot_count, dtype=bool))
    contrib = jnp.where(keep, jnp.exp(logits), 0.0)
    per_block = contrib.reshape(slot_count, remote_blocks, 128).sum(axis=2)
    named = first_block + jnp.arange(remote_blocks, dtype=jnp.int32)
    counts = jnp.sum(step_pairs[:, :, None] == named, axis=1).astype(jnp.float32)
    per_block = per_block.reshape(block_count, 128, remote_blocks)
    return jnp.sum(per_block * counts[:, None, :], axis=2)


def pack(held, held_ids):
    feature_span = held.shape[1]
    id_rows = jnp.pad(held_ids.astype(jnp.bfloat16), (0, ID_ROWS * feature_span - held_ids.shape[0]))
    return jnp.concatenate([held, id_rows.reshape(ID_ROWS, feature_span)], axis=0)


def unpack(packed):
    slot_count = packed.shape[0] - ID_ROWS
    return packed[:slot_count], packed[slot_count:].reshape(-1)[:slot_count].astype(jnp.int32)


def body(embeddings, owners, clusters, pairs):
    device_count = lax.axis_size("blk")
    row_count, feature_span = embeddings.shape
    slot_count = SLOTS
    capacity = slot_count // device_count
    block_count = slot_count // 128
    pos2dev = ring_order(device_count)
    dev2pos = np.argsort(np.asarray(pos2dev)).astype(np.int32)
    position = jnp.asarray(dev2pos)[lax.axis_index("blk")]
    odd = (position % 2) == 1

    value_entries = embeddings.astype(jnp.float32)
    unit = (
        value_entries
        * lax.rsqrt(jnp.mean(value_entries * value_entries, axis=1, keepdims=True) + 1e-06)
    ).astype(jnp.bfloat16)
    row_index = jnp.arange(row_count, dtype=jnp.int32)
    earlier = (owners[None, :] == owners[:, None]) & (row_index[None, :] < row_index[:, None])
    arrival = jnp.sum(earlier.astype(jnp.int32), axis=1)
    place = jnp.asarray(np.asarray(pos2dev, np.int32))[owners] * capacity + arrival
    slot_index = jnp.arange(slot_count, dtype=jnp.int32)
    hit = place[None, :] == slot_index[:, None]
    outgoing = jnp.dot(
        hit.astype(jnp.bfloat16), unit, preferred_element_type=jnp.float32
    ).astype(jnp.bfloat16)
    outgoing_ids = jnp.sum(jnp.where(hit, clusters[None, :] + 1, 0), axis=1) - 1
    pair_count = pairs[0].size
    side = jnp.concatenate(
        [
            outgoing_ids.reshape(device_count, capacity),
            jnp.broadcast_to(pairs[0].reshape(1, pair_count), (device_count, pair_count)),
        ],
        axis=1,
    ).astype(jnp.bfloat16)
    id_row = jnp.pad(side, ((0, 0), (0, feature_span - capacity - pair_count)))[:, None, :]
    payload = jnp.concatenate([outgoing.reshape(device_count, capacity, feature_span), id_row], axis=1)
    arrived = lax.all_to_all(payload, "blk", split_axis=0, concat_axis=0, tiled=True)
    own = arrived[:, :capacity].reshape(slot_count, feature_span)
    own_ids = arrived[:, capacity, :capacity].reshape(slot_count).astype(jnp.int32)

    all_pairs = (
        arrived[:, capacity, capacity : capacity + pair_count].astype(jnp.int32).reshape((device_count,) + pairs.shape[1:])
    )
    my_pairs = all_pairs[position]
    ahead_pairs = all_pairs[(position + 2) % device_count]

    n = device_count
    evens = range(0, n, 2)
    half = slot_count // 2
    forward = [(p, (p + 2) % n) for p in range(n)]
    swap = [(p, p ^ 1) for p in range(n)]
    lead_half = pack(own[:half], own_ids)
    fwd_a = moved(lead_half, pos2dev, forward)
    across_a = moved(lead_half, pos2dev, [(p, p + 1) for p in evens])
    across_b = moved(own[half:], pos2dev, [(p, p + 1) for p in evens])
    total = step_total(own, own_ids, own, own_ids, my_pairs[0], True)
    total, across_a, across_b = lax.optimization_barrier((total, across_a, across_b))
    across_held = jnp.concatenate([across_a[:half], across_b], axis=0)
    across_ids = across_a[half:].reshape(-1)[:slot_count].astype(jnp.int32)
    from_across = [
        step_total(own, own_ids, across_held[lo : lo + half], across_ids[lo : lo + half], my_pairs[1], False, lo // 128)
        for lo in (0, half)
    ]
    total, fwd_a, from_across = lax.optimization_barrier((total, fwd_a, from_across))
    _, second_half, packed = lax.optimization_barrier((fwd_a, own[half:], pack(own, own_ids)))
    fwd_b = moved(second_half, pos2dev, forward)
    back2 = moved(packed, pos2dev, [(p, (p - 2) % n) for p in evens] + [(p, p) for p in range(1, n, 2)])
    swapped_a = moved(fwd_a, pos2dev, swap)

    def all_ids(packed_half):
        return packed_half[half:].reshape(-1)[:slot_count].astype(jnp.int32)

    fwd_all_ids = all_ids(fwd_a)
    swapped_all_ids = all_ids(swapped_a)

    def half_steps(fwd, swapped, lo, total):
        fwd_held, fwd_ids = fwd[:half], fwd_all_ids[lo : lo + half]
        swapped_held, swapped_ids = swapped[:half], swapped_all_ids[lo : lo + half]
        q0 = lo // 128
        total = total + step_total(own, own_ids, fwd_held, fwd_ids, my_pairs[2], False, q0)
        from_swap = step_total(own, own_ids, swapped_held, swapped_ids, my_pairs[1], False, q0)
        return total + jnp.where(odd, from_across[lo // half], from_swap)

    def last_step(swapped, lo):
        back2_held, back2_ids = unpack(back2)
        swapped_held, swapped_ids = swapped[:half], swapped_all_ids[lo : lo + half]
        return step_total(
            back2_held,
            back2_ids,
            swapped_held,
            swapped_ids,
            jnp.where(odd, my_pairs[3], ahead_pairs[3]),
            False,
            lo // 128,
        )

    total = half_steps(fwd_a, swapped_a, 0, total)
    fwd_b, total = lax.optimization_barrier((fwd_b, total))
    swapped_b = moved(fwd_b, pos2dev, swap)
    total = half_steps(fwd_b, swapped_b, half, total)
    last = last_step(swapped_a, 0) + last_step(swapped_b, half)
    total = total + jnp.where(odd, last, 0.0)
    forward_part = jnp.where(odd, 0.0, last)
    totals = jnp.stack([total.reshape(device_count, capacity), forward_part.reshape(device_count, capacity)], axis=1)
    returned = lax.all_to_all(totals, "blk", split_axis=0, concat_axis=0, tiled=True)
    behind = jnp.asarray(np.asarray(pos2dev, np.int32))[(owners - 2) % device_count] * capacity + arrival
    behind = jnp.where(owners % 2 == 0, behind, -1)
    both = jnp.sum(
        jnp.where(place[:, None] == slot_index[None, :], returned[:, 0].reshape(-1)[None, :], 0.0)
        + jnp.where(behind[:, None] == slot_index[None, :], returned[:, 1].reshape(-1)[None, :], 0.0),
        axis=1,
    )
    return jnp.log1p(both)


def solution(mesh):
    placed = (
        P(("groups", "blk"), None),
        P(("groups", "blk")),
        P(("groups", "blk")),
        P(("groups", "blk"), None, None, None),
    )
    return jax.shard_map(
        body, mesh=mesh, in_specs=placed, out_specs=P(("groups", "blk")), check_vma=False
    )
```

```python
import numpy as np
import jax
import jax.numpy as jnp
from jax import lax
from jax.sharding import PartitionSpec as P

SLOTS = 1024
STEPS = 4
ID_ROWS = 16


SHARPNESS_KNOB = 32.0


def ring_order(n):
    if n == 16:
        chips = [(z, 0) for z in range(4)] + [(z, 1) for z in reversed(range(4))]
        return [chips[p // 2][0] * 4 + chips[p // 2][1] * 2 + p % 2 for p in range(n)]
    return list(range(n))


def moved(x, pos2dev, moves):
    return lax.ppermute(x, "blk", [(pos2dev[a], pos2dev[b]) for a, b in moves])


def step_total(local, local_ids, remote, remote_ids, step_pairs, first_step, first_block=0):
    slot_count, feature_span = local.shape
    block_count = slot_count // 128
    remote_blocks = remote.shape[0] // 128
    logits = lax.dot_general(
        local, remote, (((1,), (1,)), ((), ())), preferred_element_type=jnp.float32
    ) * (SHARPNESS_KNOB / feature_span)
    keep = (local_ids[:, None] == remote_ids[None, :]) & (local_ids[:, None] >= 0)
    if first_step:
        keep = keep & jnp.logical_not(jnp.eye(slot_count, dtype=bool))
    contrib = jnp.where(keep, jnp.exp(logits), 0.0)
    per_block = contrib.reshape(slot_count, remote_blocks, 128).sum(axis=2)
    named = first_block + jnp.arange(remote_blocks, dtype=jnp.int32)
    counts = jnp.sum(step_pairs[:, :, None] == named, axis=1).astype(jnp.float32)
    per_block = per_block.reshape(block_count, 128, remote_blocks)
    return jnp.sum(per_block * counts[:, None, :], axis=2)


def pack(held, held_ids):
    feature_span = held.shape[1]
    id_rows = jnp.pad(held_ids.astype(jnp.bfloat16), (0, ID_ROWS * feature_span - held_ids.shape[0]))
    return jnp.concatenate([held, id_rows.reshape(ID_ROWS, feature_span)], axis=0)


def unpack(packed):
    slot_count = packed.shape[0] - ID_ROWS
    return packed[:slot_count], packed[slot_count:].reshape(-1)[:slot_count].astype(jnp.int32)


def body(embeddings, owners, clusters, pairs):
    device_count = lax.axis_size("blk")
    row_count, feature_span = embeddings.shape
    slot_count = SLOTS
    capacity = slot_count // device_count
    block_count = slot_count // 128
    pos2dev = ring_order(device_count)
    dev2pos = np.argsort(np.asarray(pos2dev)).astype(np.int32)
    position = jnp.asarray(dev2pos)[lax.axis_index("blk")]
    odd = (position % 2) == 1

    value_entries = embeddings.astype(jnp.float32)
    unit = (
        value_entries
        * lax.rsqrt(jnp.mean(value_entries * value_entries, axis=1, keepdims=True) + 1e-06)
    ).astype(jnp.bfloat16)
    row_index = jnp.arange(row_count, dtype=jnp.int32)
    earlier = (owners[None, :] == owners[:, None]) & (row_index[None, :] < row_index[:, None])
    arrival = jnp.sum(earlier.astype(jnp.int32), axis=1)
    place = jnp.asarray(np.asarray(pos2dev, np.int32))[owners] * capacity + arrival
    slot_index = jnp.arange(slot_count, dtype=jnp.int32)
    hit = place[None, :] == slot_index[:, None]
    outgoing = jnp.dot(
        hit.astype(jnp.bfloat16), unit, preferred_element_type=jnp.float32
    ).astype(jnp.bfloat16)
    outgoing_ids = jnp.sum(jnp.where(hit, clusters[None, :] + 1, 0), axis=1) - 1
    pair_count = pairs[0].size
    side = jnp.concatenate(
        [
            outgoing_ids.reshape(device_count, capacity),
            jnp.broadcast_to(pairs[0].reshape(1, pair_count), (device_count, pair_count)),
        ],
        axis=1,
    ).astype(jnp.bfloat16)
    id_row = jnp.pad(side, ((0, 0), (0, feature_span - capacity - pair_count)))[:, None, :]
    payload = jnp.concatenate([outgoing.reshape(device_count, capacity, feature_span), id_row], axis=1)
    arrived = lax.all_to_all(payload, "blk", split_axis=0, concat_axis=0, tiled=True)
    own = arrived[:, :capacity].reshape(slot_count, feature_span)
    own_ids = arrived[:, capacity, :capacity].reshape(slot_count).astype(jnp.int32)

    all_pairs = (
        arrived[:, capacity, capacity : capacity + pair_count].astype(jnp.int32).reshape((device_count,) + pairs.shape[1:])
    )
    my_pairs = all_pairs[position]
    ahead_pairs = all_pairs[(position + 2) % device_count]

    n = device_count
    evens = range(0, n, 2)
    half = slot_count // 2
    forward = [(p, (p + 2) % n) for p in range(n)]
    swap = [(p, p ^ 1) for p in range(n)]
    lead_half = pack(own[:half], own_ids)
    fwd_a = moved(lead_half, pos2dev, forward)
    across_a = moved(lead_half, pos2dev, [(p, p + 1) for p in evens])
    across_b = moved(own[half:], pos2dev, [(p, p + 1) for p in evens])
    total = step_total(own, own_ids, own, own_ids, my_pairs[0], True)
    total, across_a, across_b = lax.optimization_barrier((total, across_a, across_b))
    across_held = jnp.concatenate([across_a[:half], across_b], axis=0)
    across_ids = across_a[half:].reshape(-1)[:slot_count].astype(jnp.int32)
    from_across = [
        step_total(own, own_ids, across_held[lo : lo + half], across_ids[lo : lo + half], my_pairs[1], False, lo // 128)
        for lo in (0, half)
    ]
    total, fwd_a, from_across = lax.optimization_barrier((total, fwd_a, from_across))
    _, second_half, packed = lax.optimization_barrier((fwd_a, own[half:], pack(own, own_ids)))
    fwd_b = moved(second_half, pos2dev, forward)
    back2 = moved(packed, pos2dev, [(p, (p - 2) % n) for p in evens] + [(p, p) for p in range(1, n, 2)])
    swapped_a = moved(fwd_a, pos2dev, swap)

    def all_ids(packed_half):
        return packed_half[half:].reshape(-1)[:slot_count].astype(jnp.int32)

    fwd_all_ids = all_ids(fwd_a)
    swapped_all_ids = all_ids(swapped_a)

    def half_steps(fwd, swapped, lo, total):
        fwd_held, fwd_ids = fwd[:half], fwd_all_ids[lo : lo + half]
        swapped_held, swapped_ids = swapped[:half], swapped_all_ids[lo : lo + half]
        q0 = lo // 128
        total = total + step_total(own, own_ids, fwd_held, fwd_ids, my_pairs[2], False, q0)
        from_swap = step_total(own, own_ids, swapped_held, swapped_ids, my_pairs[1], False, q0)
        return total + jnp.where(odd, from_across[lo // half], from_swap)

    def last_step(swapped, lo):
        back2_held, back2_ids = unpack(back2)
        swapped_held, swapped_ids = swapped[:half], swapped_all_ids[lo : lo + half]
        return step_total(
            back2_held,
            back2_ids,
            swapped_held,
            swapped_ids,
            jnp.where(odd, my_pairs[3], ahead_pairs[3]),
            False,
            lo // 128,
        )

    total = half_steps(fwd_a, swapped_a, 0, total)
    fwd_b, total = lax.optimization_barrier((fwd_b, total))
    swapped_b = moved(fwd_b, pos2dev, swap)
    total = half_steps(fwd_b, swapped_b, half, total)
    last = last_step(swapped_a, 0) + last_step(swapped_b, half)
    total = total + jnp.where(odd, last, 0.0)
    forward_part = jnp.where(odd, 0.0, last)
    totals = jnp.stack([total.reshape(device_count, capacity), forward_part.reshape(device_count, capacity)], axis=1)
    returned = lax.all_to_all(totals, "blk", split_axis=0, concat_axis=0, tiled=True)
    ring_dev = jnp.asarray(np.asarray(pos2dev, np.int32))
    source_dev = jnp.stack([ring_dev[owners], jnp.where(owners % 2 == 0, ring_dev[(owners - 2) % device_count], -1)], axis=1)
    dev_pick = (source_dev[:, :, None] == jnp.arange(device_count, dtype=jnp.int32)).astype(jnp.float32)
    by_row = jnp.einsum("rpe,epa->ra", dev_pick, returned, precision=lax.Precision.HIGHEST)
    slot_in = jnp.arange(capacity, dtype=jnp.int32)
    both = jnp.sum(jnp.where(arrival[:, None] == slot_in[None, :], by_row, 0.0), axis=1)
    return jnp.log1p(both)


def solution(mesh):
    placed = (
        P(("groups", "blk"), None),
        P(("groups", "blk")),
        P(("groups", "blk")),
        P(("groups", "blk"), None, None, None),
    )
    return jax.shard_map(
        body, mesh=mesh, in_specs=placed, out_specs=P(("groups", "blk")), check_vma=False
    )
```

```python
import numpy as np
import jax
import jax.numpy as jnp
from jax import lax
from jax.sharding import PartitionSpec as P

SLOTS = 1024
STEPS = 4
ID_ROWS = 16


SHARPNESS_KNOB = 32.0


def ring_order(n):
    if n == 16:
        chips = [(z, 0) for z in range(4)] + [(z, 1) for z in reversed(range(4))]
        return [chips[p // 2][0] * 4 + chips[p // 2][1] * 2 + p % 2 for p in range(n)]
    return list(range(n))


def moved(x, pos2dev, moves):
    return lax.ppermute(x, "blk", [(pos2dev[a], pos2dev[b]) for a, b in moves])


def step_total(local, local_ids, remote, remote_ids, step_pairs, first_step, first_block=0):
    slot_count, feature_span = local.shape
    block_count = slot_count // 128
    remote_blocks = remote.shape[0] // 128
    logits = lax.dot_general(
        local, remote, (((1,), (1,)), ((), ())), preferred_element_type=jnp.float32
    ) * (SHARPNESS_KNOB / feature_span)
    keep = (local_ids[:, None] == remote_ids[None, :]) & (local_ids[:, None] >= 0)
    if first_step:
        keep = keep & jnp.logical_not(jnp.eye(slot_count, dtype=bool))
    contrib = jnp.where(keep, jnp.exp(logits), 0.0)
    per_block = contrib.reshape(slot_count, remote_blocks, 128).sum(axis=2)
    named = first_block + jnp.arange(remote_blocks, dtype=jnp.int32)
    counts = jnp.sum(step_pairs[:, :, None] == named, axis=1).astype(jnp.float32)
    per_block = per_block.reshape(block_count, 128, remote_blocks)
    return jnp.sum(per_block * counts[:, None, :], axis=2)


def pack(held, held_ids):
    feature_span = held.shape[1]
    id_rows = jnp.pad(held_ids.astype(jnp.bfloat16), (0, ID_ROWS * feature_span - held_ids.shape[0]))
    return jnp.concatenate([held, id_rows.reshape(ID_ROWS, feature_span)], axis=0)


def unpack(packed):
    slot_count = packed.shape[0] - ID_ROWS
    return packed[:slot_count], packed[slot_count:].reshape(-1)[:slot_count].astype(jnp.int32)


def body(embeddings, owners, clusters, pairs):
    device_count = lax.axis_size("blk")
    row_count, feature_span = embeddings.shape
    slot_count = SLOTS
    capacity = slot_count // device_count
    block_count = slot_count // 128
    pos2dev = ring_order(device_count)
    dev2pos = np.argsort(np.asarray(pos2dev)).astype(np.int32)
    position = jnp.asarray(dev2pos)[lax.axis_index("blk")]
    odd = (position % 2) == 1

    value_entries = embeddings.astype(jnp.float32)
    unit = (
        value_entries
        * lax.rsqrt(jnp.mean(value_entries * value_entries, axis=1, keepdims=True) + 1e-06)
    ).astype(jnp.bfloat16)
    row_index = jnp.arange(row_count, dtype=jnp.int32)
    earlier = (owners[None, :] == owners[:, None]) & (row_index[None, :] < row_index[:, None])
    arrival = jnp.sum(earlier.astype(jnp.int32), axis=1)
    place = jnp.asarray(np.asarray(pos2dev, np.int32))[owners] * capacity + arrival
    slot_index = jnp.arange(slot_count, dtype=jnp.int32)
    hit = place[None, :] == slot_index[:, None]
    outgoing = jnp.dot(
        hit.astype(jnp.bfloat16), unit, preferred_element_type=jnp.float32
    ).astype(jnp.bfloat16)
    outgoing_ids = jnp.sum(jnp.where(hit, clusters[None, :] + 1, 0), axis=1) - 1
    pair_count = pairs[0].size
    side = jnp.concatenate(
        [
            outgoing_ids.reshape(device_count, capacity),
            jnp.broadcast_to(pairs[0].reshape(1, pair_count), (device_count, pair_count)),
        ],
        axis=1,
    ).astype(jnp.bfloat16)
    id_row = jnp.pad(side, ((0, 0), (0, feature_span - capacity - pair_count)))[:, None, :]
    payload = jnp.concatenate([outgoing.reshape(device_count, capacity, feature_span), id_row], axis=1)
    arrived = lax.all_to_all(payload, "blk", split_axis=0, concat_axis=0, tiled=True)
    own = arrived[:, :capacity].reshape(slot_count, feature_span)
    own_ids = arrived[:, capacity, :capacity].reshape(slot_count).astype(jnp.int32)

    all_pairs = (
        arrived[:, capacity, capacity : capacity + pair_count].astype(jnp.int32).reshape((device_count,) + pairs.shape[1:])
    )
    my_pairs = all_pairs[position]
    ahead_pairs = all_pairs[(position + 2) % device_count]

    n = device_count
    evens = range(0, n, 2)
    half = slot_count // 2
    forward = [(p, (p + 2) % n) for p in range(n)]
    swap = [(p, p ^ 1) for p in range(n)]
    lead_half = pack(own[:half], own_ids)
    fwd_a = moved(lead_half, pos2dev, forward)
    across_a = moved(lead_half, pos2dev, [(p, p + 1) for p in evens])
    across_b = moved(own[half:], pos2dev, [(p, p + 1) for p in evens])
    total = step_total(own, own_ids, own, own_ids, my_pairs[0], True)
    total, across_a, across_b = lax.optimization_barrier((total, across_a, across_b))
    across_held = jnp.concatenate([across_a[:half], across_b], axis=0)
    across_ids = across_a[half:].reshape(-1)[:slot_count].astype(jnp.int32)
    from_across = [
        step_total(own, own_ids, across_held[lo : lo + half], across_ids[lo : lo + half], my_pairs[1], False, lo // 128)
        for lo in (0, half)
    ]
    total, fwd_a, from_across = lax.optimization_barrier((total, fwd_a, from_across))
    _, second_half, packed = lax.optimization_barrier((fwd_a, own[half:], pack(own, own_ids)))
    fwd_b = moved(second_half, pos2dev, forward)
    back2 = moved(packed, pos2dev, [(p, (p - 2) % n) for p in evens] + [(p, p) for p in range(1, n, 2)])
    swapped_a = moved(fwd_a, pos2dev, swap)

    def all_ids(packed_half):
        return packed_half[half:].reshape(-1)[:slot_count].astype(jnp.int32)

    fwd_all_ids = all_ids(fwd_a)
    swapped_all_ids = all_ids(swapped_a)

    def half_steps(fwd, swapped, lo, total):
        fwd_held, fwd_ids = fwd[:half], fwd_all_ids[lo : lo + half]
        swapped_held, swapped_ids = swapped[:half], swapped_all_ids[lo : lo + half]
        q0 = lo // 128
        total = total + step_total(own, own_ids, fwd_held, fwd_ids, my_pairs[2], False, q0)
        from_swap = step_total(own, own_ids, swapped_held, swapped_ids, my_pairs[1], False, q0)
        return total + jnp.where(odd, from_across[lo // half], from_swap)

    def last_step(swapped, lo):
        back2_held, back2_ids = unpack(back2)
        swapped_held, swapped_ids = swapped[:half], swapped_all_ids[lo : lo + half]
        return step_total(
            back2_held,
            back2_ids,
            swapped_held,
            swapped_ids,
            jnp.where(odd, my_pairs[3], ahead_pairs[3]),
            False,
            lo // 128,
        )

    total = half_steps(fwd_a, swapped_a, 0, total)
    fwd_b, total = lax.optimization_barrier((fwd_b, total))
    swapped_b = moved(fwd_b, pos2dev, swap)
    total = half_steps(fwd_b, swapped_b, half, total)
    last = last_step(swapped_a, 0) + last_step(swapped_b, half)
    total = total + jnp.where(odd, last, 0.0)
    forward_part = jnp.where(odd, 0.0, last)
    totals = jnp.stack([total.reshape(device_count, capacity), forward_part.reshape(device_count, capacity)], axis=1).reshape(device_count, 1, 2 * capacity)
    returned = lax.all_to_all(totals, "blk", split_axis=0, concat_axis=0, tiled=True)
    ring_dev = jnp.asarray(np.asarray(pos2dev, np.int32))
    dev_index = jnp.arange(device_count, dtype=jnp.int32)
    own_dev = (ring_dev[owners][:, None] == dev_index).astype(jnp.float32)
    behind_dev = jnp.where(owners % 2 == 0, ring_dev[(owners - 2) % device_count], -1)
    behind_dev = (behind_dev[:, None] == dev_index).astype(jnp.float32)
    flat = returned.reshape(device_count, 1, 2 * capacity)
    from_owner = jnp.einsum("re,eok->rk", own_dev, flat, precision=lax.Precision.HIGHEST)
    from_behind = jnp.einsum("re,eok->rk", behind_dev, flat, precision=lax.Precision.HIGHEST)
    column = jnp.arange(2 * capacity, dtype=jnp.int32)[None, :]
    both = jnp.sum(
        jnp.where(column == arrival[:, None], from_owner, 0.0)
        + jnp.where(column == arrival[:, None] + capacity, from_behind, 0.0),
        axis=1,
    )
    return jnp.log1p(both)


def solution(mesh):
    placed = (
        P(("groups", "blk"), None),
        P(("groups", "blk")),
        P(("groups", "blk")),
        P(("groups", "blk"), None, None, None),
    )
    return jax.shard_map(
        body, mesh=mesh, in_specs=placed, out_specs=P(("groups", "blk")), check_vma=False
    )
```

```python
import numpy as np
import jax
import jax.numpy as jnp
from jax import lax
from jax.sharding import PartitionSpec as P

SLOTS = 1024
STEPS = 4
ID_ROWS = 16


SHARPNESS_KNOB = 32.0


def ring_order(n):
    if n == 16:
        chips = [(z, 0) for z in range(4)] + [(z, 1) for z in reversed(range(4))]
        return [chips[p // 2][0] * 4 + chips[p // 2][1] * 2 + p % 2 for p in range(n)]
    return list(range(n))


def moved(x, pos2dev, moves):
    return lax.ppermute(x, "blk", [(pos2dev[a], pos2dev[b]) for a, b in moves])


def step_total(local, local_ids, remote, remote_ids, step_pairs, first_step, first_block=0):
    slot_count, feature_span = local.shape
    block_count = slot_count // 128
    remote_blocks = remote.shape[0] // 128
    logits = lax.dot_general(
        local, remote, (((1,), (1,)), ((), ())), preferred_element_type=jnp.float32
    ) * (SHARPNESS_KNOB / feature_span)
    keep = (local_ids[:, None] == remote_ids[None, :]) & (local_ids[:, None] >= 0)
    if first_step:
        keep = keep & jnp.logical_not(jnp.eye(slot_count, dtype=bool))
    contrib = jnp.where(keep, jnp.exp(logits), 0.0)
    per_block = contrib.reshape(slot_count, remote_blocks, 128).sum(axis=2)
    named = first_block + jnp.arange(remote_blocks, dtype=jnp.int32)
    counts = jnp.sum(step_pairs[:, :, None] == named, axis=1).astype(jnp.float32)
    per_block = per_block.reshape(block_count, 128, remote_blocks)
    return jnp.sum(per_block * counts[:, None, :], axis=2)


def pack(held, held_ids):
    feature_span = held.shape[1]
    id_rows = jnp.pad(held_ids.astype(jnp.bfloat16), (0, ID_ROWS * feature_span - held_ids.shape[0]))
    return jnp.concatenate([held, id_rows.reshape(ID_ROWS, feature_span)], axis=0)


def unpack(packed):
    slot_count = packed.shape[0] - ID_ROWS
    return packed[:slot_count], packed[slot_count:].reshape(-1)[:slot_count].astype(jnp.int32)


def body(embeddings, owners, clusters, pairs):
    device_count = lax.axis_size("blk")
    row_count, feature_span = embeddings.shape
    slot_count = SLOTS
    capacity = slot_count // device_count
    block_count = slot_count // 128
    pos2dev = ring_order(device_count)
    dev2pos = np.argsort(np.asarray(pos2dev)).astype(np.int32)
    position = jnp.asarray(dev2pos)[lax.axis_index("blk")]
    odd = (position % 2) == 1

    value_entries = embeddings.astype(jnp.float32)
    unit = (
        value_entries
        * lax.rsqrt(jnp.mean(value_entries * value_entries, axis=1, keepdims=True) + 1e-06)
    ).astype(jnp.bfloat16)
    row_index = jnp.arange(row_count, dtype=jnp.int32)
    owner_hot = (owners[:, None] == jnp.arange(device_count, dtype=jnp.int32)).astype(jnp.bfloat16)
    before = (row_index[None, :] < row_index[:, None]).astype(jnp.bfloat16)
    prior = jnp.dot(before, owner_hot, preferred_element_type=jnp.float32)
    arrival = jnp.sum(prior * owner_hot.astype(jnp.float32), axis=1).astype(jnp.int32)
    place = jnp.asarray(np.asarray(pos2dev, np.int32))[owners] * capacity + arrival
    slot_index = jnp.arange(slot_count, dtype=jnp.int32)
    hit = place[None, :] == slot_index[:, None]
    outgoing = jnp.dot(
        hit.astype(jnp.bfloat16), unit, preferred_element_type=jnp.float32
    ).astype(jnp.bfloat16)
    outgoing_ids = jnp.sum(jnp.where(hit, clusters[None, :] + 1, 0), axis=1) - 1
    pair_count = pairs[0].size
    side = jnp.concatenate(
        [
            outgoing_ids.reshape(device_count, capacity),
            jnp.broadcast_to(pairs[0].reshape(1, pair_count), (device_count, pair_count)),
        ],
        axis=1,
    ).astype(jnp.bfloat16)
    id_row = jnp.pad(side, ((0, 0), (0, feature_span - capacity - pair_count)))[:, None, :]
    payload = jnp.concatenate([outgoing.reshape(device_count, capacity, feature_span), id_row], axis=1)
    arrived = lax.all_to_all(payload, "blk", split_axis=0, concat_axis=0, tiled=True)
    own = arrived[:, :capacity].reshape(slot_count, feature_span)
    own_ids = arrived[:, capacity, :capacity].reshape(slot_count).astype(jnp.int32)

    all_pairs = (
        arrived[:, capacity, capacity : capacity + pair_count].astype(jnp.int32).reshape((device_count,) + pairs.shape[1:])
    )
    my_pairs = all_pairs[position]
    ahead_pairs = all_pairs[(position + 2) % device_count]

    n = device_count
    evens = range(0, n, 2)
    half = slot_count // 2
    forward = [(p, (p + 2) % n) for p in range(n)]
    swap = [(p, p ^ 1) for p in range(n)]
    lead_half = pack(own[:half], own_ids)
    fwd_a = moved(lead_half, pos2dev, forward)
    across_a = moved(lead_half, pos2dev, [(p, p + 1) for p in evens])
    across_b = moved(own[half:], pos2dev, [(p, p + 1) for p in evens])
    total = step_total(own, own_ids, own, own_ids, my_pairs[0], True)
    total, across_a, across_b = lax.optimization_barrier((total, across_a, across_b))
    across_held = jnp.concatenate([across_a[:half], across_b], axis=0)
    across_ids = across_a[half:].reshape(-1)[:slot_count].astype(jnp.int32)
    from_across = [
        step_total(own, own_ids, across_held[lo : lo + half], across_ids[lo : lo + half], my_pairs[1], False, lo // 128)
        for lo in (0, half)
    ]
    total, fwd_a, from_across = lax.optimization_barrier((total, fwd_a, from_across))
    _, second_half, packed = lax.optimization_barrier((fwd_a, own[half:], pack(own, own_ids)))
    fwd_b = moved(second_half, pos2dev, forward)
    back2 = moved(packed, pos2dev, [(p, (p - 2) % n) for p in evens] + [(p, p) for p in range(1, n, 2)])
    swapped_a = moved(fwd_a, pos2dev, swap)

    def all_ids(packed_half):
        return packed_half[half:].reshape(-1)[:slot_count].astype(jnp.int32)

    fwd_all_ids = all_ids(fwd_a)
    swapped_all_ids = all_ids(swapped_a)

    def half_steps(fwd, swapped, lo, total):
        fwd_held, fwd_ids = fwd[:half], fwd_all_ids[lo : lo + half]
        swapped_held, swapped_ids = swapped[:half], swapped_all_ids[lo : lo + half]
        q0 = lo // 128
        total = total + step_total(own, own_ids, fwd_held, fwd_ids, my_pairs[2], False, q0)
        from_swap = step_total(own, own_ids, swapped_held, swapped_ids, my_pairs[1], False, q0)
        return total + jnp.where(odd, from_across[lo // half], from_swap)

    def last_step(swapped, lo):
        back2_held, back2_ids = unpack(back2)
        swapped_held, swapped_ids = swapped[:half], swapped_all_ids[lo : lo + half]
        return step_total(
            back2_held,
            back2_ids,
            swapped_held,
            swapped_ids,
            jnp.where(odd, my_pairs[3], ahead_pairs[3]),
            False,
            lo // 128,
        )

    total = half_steps(fwd_a, swapped_a, 0, total)
    fwd_b, total = lax.optimization_barrier((fwd_b, total))
    swapped_b = moved(fwd_b, pos2dev, swap)
    total = half_steps(fwd_b, swapped_b, half, total)
    last = last_step(swapped_a, 0) + last_step(swapped_b, half)
    total = total + jnp.where(odd, last, 0.0)
    forward_part = jnp.where(odd, 0.0, last)
    totals = jnp.stack([total.reshape(device_count, capacity), forward_part.reshape(device_count, capacity)], axis=1).reshape(device_count, 1, 2 * capacity)
    returned = lax.all_to_all(totals, "blk", split_axis=0, concat_axis=0, tiled=True)
    ring_dev = jnp.asarray(np.asarray(pos2dev, np.int32))
    dev_index = jnp.arange(device_count, dtype=jnp.int32)
    own_dev = (ring_dev[owners][:, None] == dev_index).astype(jnp.float32)
    behind_dev = jnp.where(owners % 2 == 0, ring_dev[(owners - 2) % device_count], -1)
    behind_dev = (behind_dev[:, None] == dev_index).astype(jnp.float32)
    flat = returned.reshape(device_count, 1, 2 * capacity)
    from_owner = jnp.einsum("re,eok->rk", own_dev, flat, precision=lax.Precision.HIGHEST)
    from_behind = jnp.einsum("re,eok->rk", behind_dev, flat, precision=lax.Precision.HIGHEST)
    column = jnp.arange(2 * capacity, dtype=jnp.int32)[None, :]
    both = jnp.sum(
        jnp.where(column == arrival[:, None], from_owner, 0.0)
        + jnp.where(column == arrival[:, None] + capacity, from_behind, 0.0),
        axis=1,
    )
    return jnp.log1p(both)


def solution(mesh):
    placed = (
        P(("groups", "blk"), None),
        P(("groups", "blk")),
        P(("groups", "blk")),
        P(("groups", "blk"), None, None, None),
    )
    return jax.shard_map(
        body, mesh=mesh, in_specs=placed, out_specs=P(("groups", "blk")), check_vma=False
    )
```

```python
import numpy as np
import jax
import jax.numpy as jnp
from jax import lax
from jax.sharding import PartitionSpec as P

SLOTS = 1024
STEPS = 4
ID_ROWS = 16


SHARPNESS_KNOB = 32.0


def ring_order(n):
    if n == 16:
        chips = [(z, 0) for z in range(4)] + [(z, 1) for z in reversed(range(4))]
        return [chips[p // 2][0] * 4 + chips[p // 2][1] * 2 + p % 2 for p in range(n)]
    return list(range(n))


def moved(x, pos2dev, moves):
    return lax.ppermute(x, "blk", [(pos2dev[a], pos2dev[b]) for a, b in moves])


def step_total(local, local_ids, remote, remote_ids, step_pairs, first_step, first_block=0):
    slot_count, feature_span = local.shape
    block_count = slot_count // 128
    remote_blocks = remote.shape[0] // 128
    logits = lax.dot_general(
        local, remote, (((1,), (1,)), ((), ())), preferred_element_type=jnp.float32
    ) * (SHARPNESS_KNOB / feature_span)
    keep = (local_ids[:, None] == remote_ids[None, :]) & (local_ids[:, None] >= 0)
    if first_step:
        keep = keep & jnp.logical_not(jnp.eye(slot_count, dtype=bool))
    contrib = jnp.where(keep, jnp.exp(logits), 0.0)
    per_block = contrib.reshape(slot_count, remote_blocks, 128).sum(axis=2)
    named = first_block + jnp.arange(remote_blocks, dtype=jnp.int32)
    counts = jnp.sum(step_pairs[:, :, None] == named, axis=1).astype(jnp.float32)
    per_block = per_block.reshape(block_count, 128, remote_blocks)
    return jnp.sum(per_block * counts[:, None, :], axis=2)


def pack(held, held_ids):
    feature_span = held.shape[1]
    id_rows = jnp.pad(held_ids.astype(jnp.bfloat16), (0, ID_ROWS * feature_span - held_ids.shape[0]))
    return jnp.concatenate([held, id_rows.reshape(ID_ROWS, feature_span)], axis=0)


def unpack(packed):
    slot_count = packed.shape[0] - ID_ROWS
    return packed[:slot_count], packed[slot_count:].reshape(-1)[:slot_count].astype(jnp.int32)


def body(embeddings, owners, clusters, pairs):
    device_count = lax.axis_size("blk")
    row_count, feature_span = embeddings.shape
    slot_count = SLOTS
    capacity = slot_count // device_count
    block_count = slot_count // 128
    pos2dev = ring_order(device_count)
    dev2pos = np.argsort(np.asarray(pos2dev)).astype(np.int32)
    position = jnp.asarray(dev2pos)[lax.axis_index("blk")]
    odd = (position % 2) == 1

    square_sum = jnp.einsum("rf,rf->r", embeddings, embeddings, preferred_element_type=jnp.float32)
    scale = lax.rsqrt(square_sum * (1.0 / feature_span) + 1e-06)
    unit = (embeddings.astype(jnp.float32) * scale[:, None]).astype(jnp.bfloat16)
    row_index = jnp.arange(row_count, dtype=jnp.int32)
    earlier = (owners[None, :] == owners[:, None]) & (row_index[None, :] < row_index[:, None])
    arrival = jnp.sum(earlier.astype(jnp.int32), axis=1)
    place = jnp.asarray(np.asarray(pos2dev, np.int32))[owners] * capacity + arrival
    slot_index = jnp.arange(slot_count, dtype=jnp.int32)
    hit = place[None, :] == slot_index[:, None]
    outgoing = jnp.dot(
        hit.astype(jnp.bfloat16), unit, preferred_element_type=jnp.float32
    ).astype(jnp.bfloat16)
    outgoing_ids = jnp.sum(jnp.where(hit, clusters[None, :] + 1, 0), axis=1) - 1
    pair_count = pairs[0].size
    side = jnp.concatenate(
        [
            outgoing_ids.reshape(device_count, capacity),
            jnp.broadcast_to(pairs[0].reshape(1, pair_count), (device_count, pair_count)),
        ],
        axis=1,
    ).astype(jnp.bfloat16)
    id_row = jnp.pad(side, ((0, 0), (0, feature_span - capacity - pair_count)))[:, None, :]
    payload = jnp.concatenate([outgoing.reshape(device_count, capacity, feature_span), id_row], axis=1)
    arrived = lax.all_to_all(payload, "blk", split_axis=0, concat_axis=0, tiled=True)
    own = arrived[:, :capacity].reshape(slot_count, feature_span)
    own_ids = arrived[:, capacity, :capacity].reshape(slot_count).astype(jnp.int32)

    all_pairs = (
        arrived[:, capacity, capacity : capacity + pair_count].astype(jnp.int32).reshape((device_count,) + pairs.shape[1:])
    )
    my_pairs = all_pairs[position]
    ahead_pairs = all_pairs[(position + 2) % device_count]

    n = device_count
    evens = range(0, n, 2)
    half = slot_count // 2
    forward = [(p, (p + 2) % n) for p in range(n)]
    swap = [(p, p ^ 1) for p in range(n)]
    lead_half = pack(own[:half], own_ids)
    fwd_a = moved(lead_half, pos2dev, forward)
    across_a = moved(lead_half, pos2dev, [(p, p + 1) for p in evens])
    across_b = moved(own[half:], pos2dev, [(p, p + 1) for p in evens])
    total = step_total(own, own_ids, own, own_ids, my_pairs[0], True)
    total, across_a, across_b = lax.optimization_barrier((total, across_a, across_b))
    across_held = jnp.concatenate([across_a[:half], across_b], axis=0)
    across_ids = across_a[half:].reshape(-1)[:slot_count].astype(jnp.int32)
    from_across = [
        step_total(own, own_ids, across_held[lo : lo + half], across_ids[lo : lo + half], my_pairs[1], False, lo // 128)
        for lo in (0, half)
    ]
    total, fwd_a, from_across = lax.optimization_barrier((total, fwd_a, from_across))
    _, second_half, packed = lax.optimization_barrier((fwd_a, own[half:], pack(own, own_ids)))
    fwd_b = moved(second_half, pos2dev, forward)
    back2 = moved(packed, pos2dev, [(p, (p - 2) % n) for p in evens] + [(p, p) for p in range(1, n, 2)])
    swapped_a = moved(fwd_a, pos2dev, swap)

    def all_ids(packed_half):
        return packed_half[half:].reshape(-1)[:slot_count].astype(jnp.int32)

    fwd_all_ids = all_ids(fwd_a)
    swapped_all_ids = all_ids(swapped_a)

    def half_steps(fwd, swapped, lo, total):
        fwd_held, fwd_ids = fwd[:half], fwd_all_ids[lo : lo + half]
        swapped_held, swapped_ids = swapped[:half], swapped_all_ids[lo : lo + half]
        q0 = lo // 128
        total = total + step_total(own, own_ids, fwd_held, fwd_ids, my_pairs[2], False, q0)
        from_swap = step_total(own, own_ids, swapped_held, swapped_ids, my_pairs[1], False, q0)
        return total + jnp.where(odd, from_across[lo // half], from_swap)

    def last_step(swapped, lo):
        back2_held, back2_ids = unpack(back2)
        swapped_held, swapped_ids = swapped[:half], swapped_all_ids[lo : lo + half]
        return step_total(
            back2_held,
            back2_ids,
            swapped_held,
            swapped_ids,
            jnp.where(odd, my_pairs[3], ahead_pairs[3]),
            False,
            lo // 128,
        )

    total = half_steps(fwd_a, swapped_a, 0, total)
    fwd_b, total = lax.optimization_barrier((fwd_b, total))
    swapped_b = moved(fwd_b, pos2dev, swap)
    total = half_steps(fwd_b, swapped_b, half, total)
    last = last_step(swapped_a, 0) + last_step(swapped_b, half)
    total = total + jnp.where(odd, last, 0.0)
    forward_part = jnp.where(odd, 0.0, last)
    totals = jnp.stack([total.reshape(device_count, capacity), forward_part.reshape(device_count, capacity)], axis=1).reshape(device_count, 1, 2 * capacity)
    returned = lax.all_to_all(totals, "blk", split_axis=0, concat_axis=0, tiled=True)
    ring_dev = jnp.asarray(np.asarray(pos2dev, np.int32))
    dev_index = jnp.arange(device_count, dtype=jnp.int32)
    own_dev = (ring_dev[owners][:, None] == dev_index).astype(jnp.float32)
    behind_dev = jnp.where(owners % 2 == 0, ring_dev[(owners - 2) % device_count], -1)
    behind_dev = (behind_dev[:, None] == dev_index).astype(jnp.float32)
    flat = returned.reshape(device_count, 1, 2 * capacity)
    from_owner = jnp.einsum("re,eok->rk", own_dev, flat, precision=lax.Precision.HIGHEST)
    from_behind = jnp.einsum("re,eok->rk", behind_dev, flat, precision=lax.Precision.HIGHEST)
    column = jnp.arange(2 * capacity, dtype=jnp.int32)[None, :]
    both = jnp.sum(
        jnp.where(column == arrival[:, None], from_owner, 0.0)
        + jnp.where(column == arrival[:, None] + capacity, from_behind, 0.0),
        axis=1,
    )
    return jnp.log1p(both)


def solution(mesh):
    placed = (
        P(("groups", "blk"), None),
        P(("groups", "blk")),
        P(("groups", "blk")),
        P(("groups", "blk"), None, None, None),
    )
    return jax.shard_map(
        body, mesh=mesh, in_specs=placed, out_specs=P(("groups", "blk")), check_vma=False
    )
```
